256 devices in a mesh: section: 2 (over core), expert: 32 (over x, z), dp: 4 (over y).
Axes of the slice: x: 4, y: 4, z: 8, core: 2. Of those that a mesh axis runs over, the one named last changes fastest.
Arguments:
- tokens: bfloat16 [2, 16384, 1024], P(None, ('expert', 'dp')), may hold values from -6 to 6
- cotangent: bfloat16 [2, 16384, 1024], P(None, ('expert', 'dp')), may hold values from -6 to 6
- routes: int32 [2, 2, 16384, 2], P('section', None, ('expert', 'dp')), may hold values from 0 to 31, all different within a row; in each aligned block of 128 rows (0 to 127, 128 to 255, ..., all dimensions but the last counted through in order) at most 12 rows name the same one
- router: bfloat16 [2, 1024, 32], P('section'), may hold values from -0.1875 to 0.1875
- w_gate: bfloat16 [2, 32, 1024, 512], P('section', 'expert'), may hold values from -0.1875 to 0.1875
- w_up: bfloat16 [2, 32, 1024, 512], P('section', 'expert'), may hold values from -0.1875 to 0.1875
- w_down: bfloat16 [2, 32, 512, 1024], P('section', 'expert'), may hold values from -0.25 to 0.25
Outputs:
- out_layers: bfloat16 [2, 2, 16384, 1024], P('section', None, ('expert', 'dp'))
- grad_in: bfloat16 [2, 2, 16384, 1024], P('section', None, ('expert', 'dp'))
- grad_gate: float32 [2, 32, 1024, 512], P('section', 'expert', 'dp')
- grad_up: float32 [2, 32, 1024, 512], P('section', 'expert', 'dp')
- grad_down: float32 [2, 32, 512, 1024], P('section', 'expert', 'dp')
- grad_router: float32 [2, 1024, 32], P('section')
The draws below stay inside these ranges and needn't reach their ends.
Inputs may be any that keep to these rules, and one draw needn't show every extreme that they name: `routes`: each token names 2 different experts. Within the tokens of one device (an aligned block of 128 tokens of one layer and micro-batch) no expert is named by more than 12 tokens, and in every draw some expert is named by exactly 12 tokens of some block.
All inputs are finite; a program needn't handle non-finite values.
Results may differ from the reference program's by a relative error of at most 0.012.
Values may be sent and summed in bfloat16 or wider, within the bound.
No kernel may reach another device: no remote copies, remote signals or barrier semaphores. Data moves between devices by JAX's collectives and lax.ppermute only.
A program may use at most 128 MiB of HBM per device.

```python
import math
import jax
import jax.numpy as jnp
import numpy as np
from jax import lax

D = 1024
FF = 512
TOP = 2
MB = 2
TOK_DEV = 128
EXPERTS = 32
LAYERS = 2
SOURCES = 32
GROUPS = 4
CAP = 12
TOKENS = 16384


def shard_levels(stream_key, extent, cuts, low, top_value):
    def one(dim, blocks):
        heights = jax.random.uniform(jax.random.fold_in(jax.random.fold_in(stream_key, 6), dim), (blocks,), jnp.float32, low / len(cuts), top_value / len(cuts))
        return jnp.repeat(jnp.exp(heights), extent[dim] // blocks).reshape((-1,) + (1,) * (len(extent) - dim - 1))

    factor_of = one(*cuts[0])
    for cut in cuts[1:]:
        factor_of = factor_of * one(*cut)
    return factor_of


def deal_out(rng, own, number, rows, count, top, reach, slope):
    order = jax.random.permutation(rng, count)
    heavy_load, usual = load_shares(count, rows * top, reach, slope, True), load_shares(count, rows * top, reach, slope, False)
    places = jnp.arange(count)

    def named(tallies, rotation):
        used = int((tallies > 0).sum())
        fixed = max(1, used // 4)
        moved = fixed + (places - fixed + rotation * (used - fixed)) % max(1, count - fixed)
        return jnp.zeros((count,), jnp.int32).at[order[jnp.where(places < fixed, places, moved)]].set(jnp.asarray(tallies, jnp.int32))

    tallies = jnp.where(number % 4 == 0, named(heavy_load, number // 4), named(usual, number - number // 4 - 1))
    mixed = jax.random.permutation(jax.random.fold_in(own, 3), count)
    giver, taker = mixed[0:count // 2 * 2:2], mixed[1:count // 2 * 2:2]
    room = jnp.minimum(tallies[giver] - 1, reach - tallies[taker]) // 2
    room = jnp.where((giver == order[0]) | (taker == order[0]) | (tallies[taker] == 0), 0, jnp.maximum(room, 0))
    moved = jax.random.randint(jax.random.fold_in(own, 4), (count // 2,), 0, 1 << 20) % (room + 1)
    tallies = tallies.at[giver].add(-moved).at[taker].add(moved)
    items = jnp.searchsorted(jnp.cumsum(tallies), jnp.arange(rows * top), side="right").astype(jnp.int32)
    table = items.reshape(top, rows).T
    table = table[jax.random.permutation(jax.random.fold_in(own, 1), rows)]
    rotation = jax.random.randint(jax.random.fold_in(own, 2), (rows, 1), 0, top)
    return jnp.take_along_axis(table, (jnp.arange(top)[None, :] + rotation) % top, axis=1)


def load_shares(amount, total, reach, lean, full):
    portions = [(1 << 20) // math.isqrt(grade ** lean) + 1 for grade in range(1, amount + 1)]
    largest = reach if full else min(reach, max(-(-total // amount), total * portions[0] // sum(portions)))
    least = 1 if total - largest >= amount - 1 else 0
    holding, spare = [largest] + [least] * (amount - 1), total - largest - least * (amount - 1)
    while spare > 0:
        candidates = [i for i in range(1, amount) if holding[i] < largest] or [i for i in range(1, amount) if holding[i] < reach]
        mass, budget = sum([portions[i] for i in candidates]), spare
        for i in candidates:
            addition = min(reach - holding[i], max(1, budget * portions[i] // mass), spare)
            holding[i] = holding[i] + addition
            spare = spare - addition
    return np.array(holding)


def noise(own_key, dims, scale, most, shards=(), held_as=jnp.bfloat16):
    array = scale * jax.random.normal(own_key, dims, jnp.float32)
    if shards:
        array = array * shard_levels(own_key, dims, shards, -0.22, 0.18)
    return jnp.clip(array, -most, most).astype(held_as)


def setup_inputs(seed: int = 0) -> dict:
    keys = jax.random.split(jax.random.key(seed), 8)
    tokens = noise(keys[0], (MB, TOKENS, D), 1.0, 6.0, ((1, 128),))
    cotangent = noise(keys[1], (MB, TOKENS, D), 1.0, 6.0, ((1, 128),))
    routes_keys = jax.random.split(jax.random.fold_in(keys[2], 1), LAYERS * MB * TOKENS // TOK_DEV)
    routes_turns = jax.random.permutation(jax.random.fold_in(keys[2], 3), LAYERS * MB * TOKENS // TOK_DEV)
    routes = jax.vmap(lambda own, number: deal_out(jax.random.fold_in(keys[2], 2), own, number, TOK_DEV, EXPERTS, TOP, CAP, 2))(routes_keys, routes_turns).reshape((LAYERS, MB, TOKENS, TOP))
    router = noise(keys[3], (LAYERS, D, EXPERTS), D ** -0.5, 0.1875, ((0, 2),))
    w_gate = noise(keys[4], (LAYERS, EXPERTS, D, FF), D ** -0.5, 0.1875, ((0, 2), (1, 32)))
    w_up = noise(keys[5], (LAYERS, EXPERTS, D, FF), D ** -0.5, 0.1875, ((0, 2), (1, 32)))
    w_down = noise(keys[6], (LAYERS, EXPERTS, FF, D), FF ** -0.5, 0.25, ((0, 2), (1, 32)))
    return {"tokens": tokens, "cotangent": cotangent, "routes": routes, "router": router, "w_gate": w_gate, "w_up": w_up, "w_down": w_down}


def contract_last(left, right):
    return lax.dot_general(left, right, (((1,), (1,)), ((), ())), preferred_element_type=jnp.float32)

def contract_first(left, right):
    return lax.dot_general(left, right, (((0,), (0,)), ((), ())), preferred_element_type=jnp.float32)

def slot_index(chosen):
    blocks = TOKENS // TOK_DEV
    flat = chosen.reshape(blocks, TOK_DEV * TOP).astype(jnp.int32)
    labels = jnp.arange(EXPERTS, dtype=jnp.int32)
    onehot = (flat[:, :, None] == labels[None, None, :]).astype(jnp.int32)
    before = jnp.cumsum(onehot, axis=1) - onehot
    position = lax.optimization_barrier(jnp.sum(before * onehot, axis=2)).astype(jnp.int32)
    block_ids = jnp.arange(blocks, dtype=jnp.int32)[:, None]
    source = block_ids // GROUPS
    group = block_ids % GROUPS
    index = (flat * GROUPS + group) * (SOURCES * CAP) + source * CAP + position
    return index.reshape(TOKENS * TOP).astype(jnp.int32)

def route_weights(hidden, chosen, router_layer):
    logits = jnp.dot(hidden, router_layer, preferred_element_type=jnp.float32)
    picked = jnp.take_along_axis(logits, chosen, axis=1)
    raised = jnp.exp(picked)
    return raised / lax.optimization_barrier(jnp.sum(raised, axis=1, keepdims=True))

def expert_forward(operands):
    rows, gate_weight, up_weight, down_weight = operands
    gate = jnp.dot(rows, gate_weight, preferred_element_type=jnp.float32)
    up_term = jnp.dot(rows, up_weight, preferred_element_type=jnp.float32)
    inner = (jax.nn.silu(gate) * up_term).astype(jnp.bfloat16)
    return jnp.dot(inner, down_weight, preferred_element_type=jnp.float32).astype(jnp.bfloat16)

def expert_backward(operands):
    rows, grad_rows, gate_weight, up_weight, down_weight = operands
    gate = jnp.dot(rows, gate_weight, preferred_element_type=jnp.float32)
    up_term = jnp.dot(rows, up_weight, preferred_element_type=jnp.float32)
    active = jax.nn.silu(gate)
    inner = (active * up_term).astype(jnp.bfloat16)
    d_hidden = contract_last(grad_rows, down_weight)
    sigma = jax.nn.sigmoid(gate)
    d_gate = (d_hidden * up_term * sigma * (1.0 + gate * (1.0 - sigma))).astype(jnp.bfloat16)
    d_up = (d_hidden * active).astype(jnp.bfloat16)
    d_rows = (contract_last(d_gate, gate_weight) + contract_last(d_up, up_weight)).astype(jnp.bfloat16)
    return (d_rows, contract_first(rows, d_gate), contract_first(rows, d_up), contract_first(inner, grad_rows))

def spread_rows(values, index):
    total = EXPERTS * GROUPS * SOURCES * CAP
    buffer = jnp.zeros((total, D), jnp.bfloat16).at[index].set(values)
    return buffer.reshape(EXPERTS, GROUPS * SOURCES * CAP, D)

def layer_forward(hidden, chosen, router_layer, gate_weight, up_weight, down_weight):
    weights = route_weights(hidden, chosen, router_layer)
    index = slot_index(chosen)
    spread = spread_rows(jnp.repeat(hidden, TOP, axis=0), index)
    results = lax.map(expert_forward, (spread, gate_weight, up_weight, down_weight))
    picked = results.reshape(-1, D)[index].reshape(TOKENS, TOP, D)
    mixed = hidden.astype(jnp.float32) + lax.optimization_barrier(jnp.sum(weights[:, :, None] * picked.astype(jnp.float32), axis=1))
    return (mixed.astype(jnp.bfloat16), picked)

def layer_backward(hidden, upstream, picked, chosen, router_layer, gate_weight, up_weight, down_weight):
    weights = route_weights(hidden, chosen, router_layer)
    index = slot_index(chosen)
    flowing = upstream.astype(jnp.float32)
    along = lax.optimization_barrier(jnp.sum(flowing[:, None, :] * picked.astype(jnp.float32), axis=2))
    grad_y = (weights[:, :, None] * flowing[:, None, :]).astype(jnp.bfloat16).reshape(TOKENS * TOP, D)
    spread = spread_rows(jnp.repeat(hidden, TOP, axis=0), index)
    grad_spread = spread_rows(grad_y, index)
    d_rows, g_gate, g_up, g_down = lax.map(expert_backward, (spread, grad_spread, gate_weight, up_weight, down_weight))
    back = d_rows.reshape(-1, D)[index].reshape(TOKENS, TOP, D)
    grad_h = flowing + lax.optimization_barrier(jnp.sum(back.astype(jnp.float32), axis=1))
    grad_s = weights * (along - lax.optimization_barrier(jnp.sum(weights * along, axis=1, keepdims=True)))
    labels = jnp.arange(EXPERTS, dtype=jnp.int32)
    match = chosen[:, :, None] == labels[None, None, :]
    grad_logits = lax.optimization_barrier(jnp.sum(jnp.where(match, grad_s[:, :, None], 0.0), axis=1)).astype(jnp.bfloat16)
    g_router = contract_first(hidden, grad_logits)
    grad_h = grad_h + contract_last(grad_logits, router_layer)
    return (grad_h.astype(jnp.bfloat16), g_gate, g_up, g_down, g_router)

def reference(tokens, cotangent, routes, router, w_gate, w_up, w_down):
    expert_scale = 1.0 / math.sqrt(MB * GROUPS * TOK_DEV * TOP)
    router_scale = 1.0 / math.sqrt(MB * TOKENS)
    inputs = [tokens[batch] for batch in range(MB)]
    saved_inputs = []
    saved_picked = []
    layer_outs = []
    for layer in range(LAYERS):
        outs = []
        picks = []
        for batch in range(MB):
            mixed, picked = layer_forward(inputs[batch], routes[layer, batch], router[layer], w_gate[layer], w_up[layer], w_down[layer])
            outs.append(mixed)
            picks.append(picked)
        saved_inputs.append(inputs)
        saved_picked.append(picks)
        layer_outs.append(jnp.stack(outs))
        inputs = outs
    upstream = [cotangent[batch] for batch in range(MB)]
    grads_in = [None] * LAYERS
    gates = [None] * LAYERS
    ups = [None] * LAYERS
    downs = [None] * LAYERS
    routers = [None] * LAYERS
    for layer in reversed(range(LAYERS)):
        passed = []
        sum_gate = jnp.zeros((EXPERTS, D, FF), jnp.float32)
        sum_up = jnp.zeros((EXPERTS, D, FF), jnp.float32)
        sum_down = jnp.zeros((EXPERTS, FF, D), jnp.float32)
        sum_router = jnp.zeros((D, EXPERTS), jnp.float32)
        for batch in range(MB):
            grad_h, g_gate, g_up, g_down, g_router = layer_backward(saved_inputs[layer][batch], upstream[batch], saved_picked[layer][batch], routes[layer, batch], router[layer], w_gate[layer], w_up[layer], w_down[layer])
            passed.append(grad_h)
            sum_gate = sum_gate + g_gate
            sum_up = sum_up + g_up
            sum_down = sum_down + g_down
            sum_router = sum_router + g_router
        grads_in[layer] = jnp.stack(passed)
        gates[layer] = sum_gate * expert_scale
        ups[layer] = sum_up * expert_scale
        downs[layer] = sum_down * expert_scale
        routers[layer] = sum_router * router_scale
        upstream = passed
    return (jnp.stack(layer_outs), jnp.stack(grads_in), jnp.stack(gates), jnp.stack(ups), jnp.stack(downs), jnp.stack(routers))
```

```python
import math

import jax
import jax.numpy as jnp
from jax import lax
from jax.sharding import PartitionSpec as P


def from_behind(array, axis, by):
    length = lax.axis_size(axis)
    pairs = [(i, i + by) for i in range(length) if 0 <= i + by < length]
    return lax.ppermute(array, axis, pairs)


def contract_last(left, right):
    return lax.dot_general(
        left, right, (((1,), (1,)), ((), ())), preferred_element_type=jnp.float32
    )


def contract_first(left, right):
    return lax.dot_general(
        left, right, (((0,), (0,)), ((), ())), preferred_element_type=jnp.float32
    )


def slot_index(chosen, experts, capacity):
    flat = chosen.reshape(-1)
    labels = jnp.arange(experts, dtype=jnp.int32)
    onehot = (flat[:, None] == labels[None, :]).astype(jnp.int32)
    before = jnp.cumsum(onehot, axis=0) - onehot
    position = jnp.sum(before * onehot, axis=1)
    return flat * capacity + position


def route_weights(hidden, chosen, router_layer):
    logits = jnp.dot(hidden, router_layer, preferred_element_type=jnp.float32)
    labels = jnp.arange(logits.shape[1], dtype=jnp.int32)
    match = chosen[:, :, None] == labels[None, None, :]
    picked = jnp.sum(jnp.where(match, logits[:, None, :], 0.0), axis=2)
    raised = jnp.exp(picked)
    return raised / jnp.sum(raised, axis=1, keepdims=True)


def expert_trade(block):
    return lax.all_to_all(block, "expert", split_axis=0, concat_axis=0, tiled=True)


def fetch(store, place):
    return lax.dynamic_index_in_dim(store, place, 0, keepdims=False)


def store_at(store, value, place, valid):
    previous = fetch(store, place)
    return lax.dynamic_update_index_in_dim(store, jnp.where(valid, value, previous), place, 0)


def group_reduce(whole_gate, whole_up, whole_down, groups):
    stacked = jnp.stack(
        [part.reshape(groups, -1) for part in (whole_gate, whole_up, whole_down)], axis=1
    ).astype(jnp.bfloat16)
    traded = lax.all_to_all(stacked, "dp", 0, 0, tiled=True)
    summed = jnp.sum(traded.astype(jnp.float32), axis=0)
    rows_gate = whole_gate.shape[0] // groups
    rows_down = whole_down.shape[0] // groups
    return (
        summed[0].reshape(rows_gate, whole_gate.shape[1]),
        summed[1].reshape(rows_gate, whole_up.shape[1]),
        summed[2].reshape(rows_down, whole_down.shape[1]),
    )


def device_reduce(value, count):
    chunks = value.reshape(count, -1, value.shape[1])
    traded = lax.all_to_all(chunks, ("expert", "dp"), 0, 0, tiled=True)
    total = jnp.sum(traded, axis=0, keepdims=True)
    spread = jnp.broadcast_to(total, chunks.shape)
    return lax.all_to_all(spread, ("expert", "dp"), 0, 0, tiled=True).reshape(value.shape)


def shards(tokens, cotangent, routes, router, w_gate, w_up, w_down):
    sections = lax.axis_size("section")
    sources = lax.axis_size("expert")
    groups = lax.axis_size("dp")
    section_id = lax.axis_index("section")
    batches, per_device, width = tokens.shape
    top = routes.shape[3]
    experts = router.shape[2]
    capacity = 3 * per_device * top // (2 * experts)
    router_layer = router[0]
    gate_weight = w_gate[0, 0]
    up_weight = w_up[0, 0]
    down_weight = w_down[0, 0]
    units = gate_weight.shape[1]
    total_rows = sources * capacity
    ticks = batches + sections - 1
    chosen_all = routes[0]
    labels = jnp.arange(experts, dtype=jnp.int32)
    kept_inputs = jnp.zeros((batches, per_device, width), jnp.bfloat16)
    kept_picked = jnp.zeros((batches, per_device * top, width), jnp.bfloat16)
    kept_rows = jnp.zeros((batches, total_rows, width), jnp.bfloat16)
    outputs = jnp.zeros((batches, per_device, width), jnp.bfloat16)
    carried = jnp.zeros((per_device, width), jnp.bfloat16)
    for tick in range(ticks):
        batch_index = tick - section_id
        valid = jnp.logical_and(batch_index >= 0, batch_index < batches)
        place = jnp.clip(batch_index, 0, batches - 1)
        fresh = tokens[tick] if tick < batches else jnp.zeros((per_device, width), jnp.bfloat16)
        hidden = jnp.where(section_id == 0, fresh, carried)
        chosen = fetch(chosen_all, place)
        weights = route_weights(hidden, chosen, router_layer)
        index = slot_index(chosen, experts, capacity)
        spread = (
            jnp.zeros((experts * capacity, width), jnp.bfloat16)
            .at[index]
            .set(jnp.repeat(hidden, top, axis=0))
        )
        arrived = expert_trade(spread.reshape(experts, capacity, width)).reshape(total_rows, width)
        gate = jnp.dot(arrived, gate_weight, preferred_element_type=jnp.float32)
        up_term = jnp.dot(arrived, up_weight, preferred_element_type=jnp.float32)
        inner = (jax.nn.silu(gate) * up_term).astype(jnp.bfloat16)
        produced = jnp.dot(inner, down_weight, preferred_element_type=jnp.float32).astype(
            jnp.bfloat16
        )
        returned = expert_trade(produced.reshape(sources, capacity, width)).reshape(
            experts * capacity, width
        )
        picked = returned[index]
        blended = jnp.sum(
            weights[:, :, None] * picked.reshape(per_device, top, width).astype(jnp.float32), axis=1
        )
        mixed = (hidden.astype(jnp.float32) + blended).astype(jnp.bfloat16)
        outputs = store_at(outputs, mixed, place, valid)
        kept_inputs = store_at(kept_inputs, hidden, place, valid)
        kept_picked = store_at(kept_picked, picked, place, valid)
        kept_rows = store_at(kept_rows, arrived, place, valid)
        if tick + 1 < ticks:
            carried = from_behind(mixed, "section", 1)
    kept_dgate = jnp.zeros((batches, total_rows, units), jnp.bfloat16)
    kept_dup = jnp.zeros((batches, total_rows, units), jnp.bfloat16)
    kept_inner = jnp.zeros((batches, total_rows, units), jnp.bfloat16)
    kept_grads = jnp.zeros((batches, total_rows, width), jnp.bfloat16)
    sum_router = jnp.zeros((width, experts), jnp.float32)
    grad_store = jnp.zeros((batches, per_device, width), jnp.bfloat16)
    carried = jnp.zeros((per_device, width), jnp.bfloat16)
    for tick in range(ticks):
        batch_index = tick - (sections - 1 - section_id)
        valid = jnp.logical_and(batch_index >= 0, batch_index < batches)
        place = jnp.clip(batch_index, 0, batches - 1)
        fresh = cotangent[tick] if tick < batches else jnp.zeros((per_device, width), jnp.bfloat16)
        upstream = jnp.where(section_id == sections - 1, fresh, carried)
        upstream = jnp.where(valid, upstream, jnp.zeros_like(upstream))
        chosen = fetch(chosen_all, place)
        hidden = fetch(kept_inputs, place)
        picked = fetch(kept_picked, place)
        arrived = fetch(kept_rows, place)
        weights = route_weights(hidden, chosen, router_layer)
        index = slot_index(chosen, experts, capacity)
        flowing = upstream.astype(jnp.float32)
        along = jnp.sum(
            flowing[:, None, :] * picked.reshape(per_device, top, width).astype(jnp.float32), axis=2
        )
        grad_y = (
            (weights[:, :, None] * flowing[:, None, :])
            .astype(jnp.bfloat16)
            .reshape(per_device * top, width)
        )
        spread = jnp.zeros((experts * capacity, width), jnp.bfloat16).at[index].set(grad_y)
        grad_rows = expert_trade(spread.reshape(experts, capacity, width)).reshape(
            total_rows, width
        )
        gate = jnp.dot(arrived, gate_weight, preferred_element_type=jnp.float32)
        up_term = jnp.dot(arrived, up_weight, preferred_element_type=jnp.float32)
        active = jax.nn.silu(gate)
        inner = (active * up_term).astype(jnp.bfloat16)
        d_hidden = contract_last(grad_rows, down_weight)
        sigma = jax.nn.sigmoid(gate)
        d_gate = (d_hidden * up_term * sigma * (1.0 + gate * (1.0 - sigma))).astype(jnp.bfloat16)
        d_up = (d_hidden * active).astype(jnp.bfloat16)
        d_rows = (contract_last(d_gate, gate_weight) + contract_last(d_up, up_weight)).astype(
            jnp.bfloat16
        )
        returned = expert_trade(d_rows.reshape(sources, capacity, width)).reshape(
            experts * capacity, width
        )
        back = returned[index].reshape(per_device, top, width)
        grad_h = flowing + jnp.sum(back.astype(jnp.float32), axis=1)
        grad_s = weights * (along - jnp.sum(weights * along, axis=1, keepdims=True))
        match = chosen[:, :, None] == labels[None, None, :]
        grad_logits = jnp.sum(jnp.where(match, grad_s[:, :, None], 0.0), axis=1).astype(
            jnp.bfloat16
        )
        local_router = contract_first(hidden, grad_logits)
        grad_h = grad_h + contract_last(grad_logits, router_layer)
        passed = grad_h.astype(jnp.bfloat16)
        grad_store = store_at(grad_store, passed, place, valid)
        kept_dgate = store_at(kept_dgate, d_gate, place, valid)
        kept_dup = store_at(kept_dup, d_up, place, valid)
        kept_inner = store_at(kept_inner, inner, place, valid)
        kept_grads = store_at(kept_grads, grad_rows, place, valid)
        sum_router = sum_router + local_router
        if tick + 1 < ticks:
            carried = from_behind(passed, "section", -1)
    all_rows = kept_rows.reshape(batches * total_rows, width)
    whole_gate = contract_first(all_rows, kept_dgate.reshape(batches * total_rows, units))
    whole_up = contract_first(all_rows, kept_dup.reshape(batches * total_rows, units))
    whole_down = contract_first(
        kept_inner.reshape(batches * total_rows, units),
        kept_grads.reshape(batches * total_rows, width),
    )
    sum_gate, sum_up, sum_down = group_reduce(whole_gate, whole_up, whole_down, groups)
    sum_router = device_reduce(sum_router, sources * groups)
    expert_scale = 1.0 / math.sqrt(batches * groups * per_device * top)
    router_scale = 1.0 / math.sqrt(batches * per_device * sources * groups)
    return (
        outputs[None],
        grad_store[None],
        (sum_gate * expert_scale)[None, None],
        (sum_up * expert_scale)[None, None],
        (sum_down * expert_scale)[None, None],
        (sum_router * router_scale)[None],
    )


def solution(mesh):
    placed = (
        P(None, ("expert", "dp"), None),
        P(None, ("expert", "dp"), None),
        P("section", None, ("expert", "dp"), None),
        P("section", None, None),
        P("section", "expert", None, None),
        P("section", "expert", None, None),
        P("section", "expert", None, None),
    )
    return jax.shard_map(
        shards,
        mesh=mesh,
        in_specs=placed,
        out_specs=(
            P("section", None, ("expert", "dp"), None),
            P("section", None, ("expert", "dp"), None),
            P("section", "expert", "dp", None),
            P("section", "expert", "dp", None),
            P("section", "expert", "dp", None),
            P("section", None, None),
        ),
        check_vma=False,
    )
```

```python
import math

import jax
import jax.numpy as jnp
from jax import lax
from jax.sharding import PartitionSpec as P


def from_behind(array, axis, by):
    length = lax.axis_size(axis)
    pairs = [(i, i + by) for i in range(length) if 0 <= i + by < length]
    return lax.ppermute(array, axis, pairs)


def contract_last(left, right):
    return lax.dot_general(
        left, right, (((1,), (1,)), ((), ())), preferred_element_type=jnp.float32
    )


def contract_first(left, right):
    return lax.dot_general(
        left, right, (((0,), (0,)), ((), ())), preferred_element_type=jnp.float32
    )


def slot_index(chosen, experts, capacity):
    flat = chosen.reshape(-1)
    labels = jnp.arange(experts, dtype=jnp.int32)
    onehot = (flat[:, None] == labels[None, :]).astype(jnp.int32)
    before = jnp.cumsum(onehot, axis=0) - onehot
    position = jnp.sum(before * onehot, axis=1)
    return flat * capacity + position


def route_weights(hidden, chosen, router_layer):
    logits = jnp.dot(hidden, router_layer, preferred_element_type=jnp.float32)
    labels = jnp.arange(logits.shape[1], dtype=jnp.int32)
    match = chosen[:, :, None] == labels[None, None, :]
    picked = jnp.sum(jnp.where(match, logits[:, None, :], 0.0), axis=2)
    raised = jnp.exp(picked)
    return raised / jnp.sum(raised, axis=1, keepdims=True)


def expert_trade(block):
    return lax.all_to_all(block, "expert", split_axis=0, concat_axis=0, tiled=True)


def fetch(store, place):
    return lax.dynamic_index_in_dim(store, place, 0, keepdims=False)


def store_at(store, value, place, valid):
    previous = fetch(store, place)
    return lax.dynamic_update_index_in_dim(store, jnp.where(valid, value, previous), place, 0)


def group_reduce(whole_gate, whole_up, whole_down, groups):
    stacked = jnp.stack(
        [part.reshape(groups, -1) for part in (whole_gate, whole_up, whole_down)], axis=1
    ).astype(jnp.bfloat16)
    traded = lax.all_to_all(stacked, "dp", 0, 0, tiled=True)
    summed = jnp.sum(traded.astype(jnp.float32), axis=0)
    rows_gate = whole_gate.shape[0] // groups
    rows_down = whole_down.shape[0] // groups
    return (
        summed[0].reshape(rows_gate, whole_gate.shape[1]),
        summed[1].reshape(rows_gate, whole_up.shape[1]),
        summed[2].reshape(rows_down, whole_down.shape[1]),
    )


def device_reduce(value, count):
    chunks = value.reshape(count, -1, value.shape[1])
    traded = lax.all_to_all(chunks, ("expert", "dp"), 0, 0, tiled=True)
    total = jnp.sum(traded, axis=0, keepdims=True)
    spread = jnp.broadcast_to(total, chunks.shape)
    return lax.all_to_all(spread, ("expert", "dp"), 0, 0, tiled=True).reshape(value.shape)


def swap(array):
    return lax.ppermute(array, "section", [(0, 1), (1, 0)])


def pick(flag, first, second):
    return jnp.where(flag, first, second)


def layer_forward(hidden, chosen, router_layer, gate_weight, up_weight, down_weight, shape):
    experts, capacity, sources, width = shape
    per_device = hidden.shape[0]
    top = chosen.shape[1]
    weights = route_weights(hidden, chosen, router_layer)
    index = slot_index(chosen, experts, capacity)
    spread = (
        jnp.zeros((experts * capacity, width), jnp.bfloat16)
        .at[index]
        .set(jnp.repeat(hidden, top, axis=0))
    )
    arrived = expert_trade(spread.reshape(experts, capacity, width)).reshape(
        sources * capacity, width
    )
    gate = jnp.dot(arrived, gate_weight, preferred_element_type=jnp.float32)
    up_term = jnp.dot(arrived, up_weight, preferred_element_type=jnp.float32)
    inner = (jax.nn.silu(gate) * up_term).astype(jnp.bfloat16)
    produced = jnp.dot(inner, down_weight, preferred_element_type=jnp.float32).astype(jnp.bfloat16)
    returned = expert_trade(produced.reshape(sources, capacity, width)).reshape(
        experts * capacity, width
    )
    picked = returned[index]
    blended = jnp.sum(
        weights[:, :, None] * picked.reshape(per_device, top, width).astype(jnp.float32), axis=1
    )
    mixed = (hidden.astype(jnp.float32) + blended).astype(jnp.bfloat16)
    return mixed, (hidden, picked, arrived, weights, index)


def layer_backward(upstream, saved, chosen, router_layer, gate_weight, up_weight, down_weight, shape):
    experts, capacity, sources, width = shape
    hidden, picked, arrived, weights, index = saved
    per_device = hidden.shape[0]
    top = chosen.shape[1]
    labels = jnp.arange(experts, dtype=jnp.int32)
    flowing = upstream.astype(jnp.float32)
    along = jnp.sum(
        flowing[:, None, :] * picked.reshape(per_device, top, width).astype(jnp.float32), axis=2
    )
    grad_y = (
        (weights[:, :, None] * flowing[:, None, :])
        .astype(jnp.bfloat16)
        .reshape(per_device * top, width)
    )
    spread = jnp.zeros((experts * capacity, width), jnp.bfloat16).at[index].set(grad_y)
    grad_rows = expert_trade(spread.reshape(experts, capacity, width)).reshape(
        sources * capacity, width
    )
    gate = jnp.dot(arrived, gate_weight, preferred_element_type=jnp.float32)
    up_term = jnp.dot(arrived, up_weight, preferred_element_type=jnp.float32)
    active = jax.nn.silu(gate)
    inner = (active * up_term).astype(jnp.bfloat16)
    d_hidden = contract_last(grad_rows, down_weight)
    sigma = jax.nn.sigmoid(gate)
    d_gate = (d_hidden * up_term * sigma * (1.0 + gate * (1.0 - sigma))).astype(jnp.bfloat16)
    d_up = (d_hidden * active).astype(jnp.bfloat16)
    d_rows = (contract_last(d_gate, gate_weight) + contract_last(d_up, up_weight)).astype(
        jnp.bfloat16
    )
    returned = expert_trade(d_rows.reshape(sources, capacity, width)).reshape(
        experts * capacity, width
    )
    back = returned[index].reshape(per_device, top, width)
    grad_h = flowing + jnp.sum(back.astype(jnp.float32), axis=1)
    grad_s = weights * (along - jnp.sum(weights * along, axis=1, keepdims=True))
    match = chosen[:, :, None] == labels[None, None, :]
    grad_logits = jnp.sum(jnp.where(match, grad_s[:, :, None], 0.0), axis=1).astype(jnp.bfloat16)
    local_router = contract_first(hidden, grad_logits)
    grad_h = grad_h + contract_last(grad_logits, router_layer)
    passed = grad_h.astype(jnp.bfloat16)
    grads = (
        contract_first(arrived, d_gate),
        contract_first(arrived, d_up),
        contract_first(inner, grad_rows),
    )
    return passed, grads, local_router


def shards(tokens, cotangent, routes, router, w_gate, w_up, w_down):
    sources = lax.axis_size("expert")
    groups = lax.axis_size("dp")
    section_id = lax.axis_index("section")
    batches, per_device, width = tokens.shape
    top = routes.shape[3]
    experts = router.shape[2]
    capacity = 3 * per_device * top // (2 * experts)
    shape = (experts, capacity, sources, width)
    layers = 2
    mine = section_id
    own = (router[0], w_gate[0, 0], w_up[0, 0], w_down[0, 0], fetch(routes[0], mine))
    other = swap((router[0], w_gate[0, 0], w_up[0, 0], w_down[0, 0], fetch(routes[0], 1 - mine)))
    params = [
        tuple(pick(section_id == layer, a, b) for a, b in zip(own, other)) for layer in range(layers)
    ]
    hidden = fetch(tokens, mine)
    outs = []
    saved = []
    for layer in range(layers):
        router_layer, gate_weight, up_weight, down_weight, chosen = params[layer]
        hidden, kept = layer_forward(
            hidden, chosen, router_layer, gate_weight, up_weight, down_weight, shape
        )
        outs.append(hidden)
        saved.append(kept)
    upstream = fetch(cotangent, mine)
    passed = [None] * layers
    grads = [None] * layers
    routers = [None] * layers
    for layer in reversed(range(layers)):
        router_layer, gate_weight, up_weight, down_weight, chosen = params[layer]
        upstream, grads[layer], routers[layer] = layer_backward(
            upstream, saved[layer], chosen, router_layer, gate_weight, up_weight, down_weight, shape
        )
        passed[layer] = upstream
    first = section_id == 0

    def place(values):
        held = pick(first, values[0], values[1])
        sent = swap(pick(first, values[1], values[0]))
        return jnp.stack([pick(first, held, sent), pick(first, sent, held)])

    out_block = place(outs)
    grad_block = place(passed)
    own_grads = tuple(pick(first, a, b) for a, b in zip(grads[0], grads[1]))
    sent_grads = swap(
        tuple(pick(first, b, a).astype(jnp.bfloat16) for a, b in zip(grads[0], grads[1]))
    )
    whole_gate, whole_up, whole_down = (
        a + b.astype(jnp.float32) for a, b in zip(own_grads, sent_grads)
    )
    sum_gate, sum_up, sum_down = group_reduce(whole_gate, whole_up, whole_down, groups)
    own_router = pick(first, routers[0], routers[1])
    sum_router = own_router + swap(pick(first, routers[1], routers[0]))
    sum_router = device_reduce(sum_router, sources * groups)
    expert_scale = 1.0 / math.sqrt(batches * groups * per_device * top)
    router_scale = 1.0 / math.sqrt(batches * per_device * sources * groups)
    return (
        out_block[None],
        grad_block[None],
        (sum_gate * expert_scale)[None, None],
        (sum_up * expert_scale)[None, None],
        (sum_down * expert_scale)[None, None],
        (sum_router * router_scale)[None],
    )


def solution(mesh):
    placed = (
        P(None, ("expert", "dp"), None),
        P(None, ("expert", "dp"), None),
        P("section", None, ("expert", "dp"), None),
        P("section", None, None),
        P("section", "expert", None, None),
        P("section", "expert", None, None),
        P("section", "expert", None, None),
    )
    return jax.shard_map(
        shards,
        mesh=mesh,
        in_specs=placed,
        out_specs=(
            P("section", None, ("expert", "dp"), None),
            P("section", None, ("expert", "dp"), None),
            P("section", "expert", "dp", None),
            P("section", "expert", "dp", None),
            P("section", "expert", "dp", None),
            P("section", None, None),
        ),
        check_vma=False,
    )
```

```python
import math

import jax
import jax.numpy as jnp
from jax import lax
from jax.sharding import PartitionSpec as P


def from_behind(array, axis, by):
    length = lax.axis_size(axis)
    pairs = [(i, i + by) for i in range(length) if 0 <= i + by < length]
    return lax.ppermute(array, axis, pairs)


def contract_last(left, right):
    return lax.dot_general(
        left, right, (((1,), (1,)), ((), ())), preferred_element_type=jnp.float32
    )


def contract_first(left, right):
    return lax.dot_general(
        left, right, (((0,), (0,)), ((), ())), preferred_element_type=jnp.float32
    )


def slot_index(chosen, experts, capacity):
    flat = chosen.reshape(-1)
    labels = jnp.arange(experts, dtype=jnp.int32)
    onehot = (flat[:, None] == labels[None, :]).astype(jnp.int32)
    before = jnp.cumsum(onehot, axis=0) - onehot
    position = jnp.sum(before * onehot, axis=1)
    return flat * capacity + position


def route_weights(hidden, chosen, router_layer):
    logits = jnp.dot(hidden, router_layer, preferred_element_type=jnp.float32)
    labels = jnp.arange(logits.shape[1], dtype=jnp.int32)
    match = chosen[:, :, None] == labels[None, None, :]
    picked = jnp.sum(jnp.where(match, logits[:, None, :], 0.0), axis=2)
    raised = jnp.exp(picked)
    return raised / jnp.sum(raised, axis=1, keepdims=True)


def expert_trade(block):
    return lax.all_to_all(block, "expert", split_axis=0, concat_axis=0, tiled=True)


def fetch(store, place):
    return lax.dynamic_index_in_dim(store, place, 0, keepdims=False)


def store_at(store, value, place, valid):
    previous = fetch(store, place)
    return lax.dynamic_update_index_in_dim(store, jnp.where(valid, value, previous), place, 0)


def group_reduce(whole_gate, whole_up, whole_down, groups):
    stacked = jnp.stack(
        [part.reshape(groups, -1) for part in (whole_gate, whole_up, whole_down)], axis=1
    ).astype(jnp.bfloat16)
    traded = lax.all_to_all(stacked, "dp", 0, 0, tiled=True)
    summed = jnp.sum(traded.astype(jnp.float32), axis=0)
    rows_gate = whole_gate.shape[0] // groups
    rows_down = whole_down.shape[0] // groups
    return (
        summed[0].reshape(rows_gate, whole_gate.shape[1]),
        summed[1].reshape(rows_gate, whole_up.shape[1]),
        summed[2].reshape(rows_down, whole_down.shape[1]),
    )


def device_reduce(value, count):
    chunks = value.reshape(count, -1, value.shape[1])
    traded = lax.all_to_all(chunks, ("expert", "dp"), 0, 0, tiled=True)
    total = jnp.sum(traded, axis=0, keepdims=True)
    spread = jnp.broadcast_to(total, chunks.shape)
    return lax.all_to_all(spread, ("expert", "dp"), 0, 0, tiled=True).reshape(value.shape)


def swap(array):
    return lax.ppermute(array, "section", [(0, 1), (1, 0)])


def pick(flag, first, second):
    return jnp.where(flag, first, second)


def layer_forward(hidden, chosen, router_layer, gate_weight, up_weight, down_weight, shape):
    experts, capacity, sources, width = shape
    per_device = hidden.shape[0]
    top = chosen.shape[1]
    weights = route_weights(hidden, chosen, router_layer)
    index = slot_index(chosen, experts, capacity)
    spread = (
        jnp.zeros((experts * capacity, width), jnp.bfloat16)
        .at[index]
        .set(jnp.repeat(hidden, top, axis=0))
    )
    arrived = expert_trade(spread.reshape(experts, capacity, width)).reshape(
        sources * capacity, width
    )
    gate = jnp.dot(arrived, gate_weight, preferred_element_type=jnp.float32)
    up_term = jnp.dot(arrived, up_weight, preferred_element_type=jnp.float32)
    inner = (jax.nn.silu(gate) * up_term).astype(jnp.bfloat16)
    produced = jnp.dot(inner, down_weight, preferred_element_type=jnp.float32).astype(jnp.bfloat16)
    returned = expert_trade(produced.reshape(sources, capacity, width)).reshape(
        experts * capacity, width
    )
    picked = returned[index]
    blended = jnp.sum(
        weights[:, :, None] * picked.reshape(per_device, top, width).astype(jnp.float32), axis=1
    )
    mixed = (hidden.astype(jnp.float32) + blended).astype(jnp.bfloat16)
    return mixed, (hidden, picked, arrived, weights, index)


def layer_backward(upstream, saved, chosen, router_layer, gate_weight, up_weight, down_weight, shape):
    experts, capacity, sources, width = shape
    hidden, picked, arrived, weights, index = saved
    per_device = hidden.shape[0]
    top = chosen.shape[1]
    labels = jnp.arange(experts, dtype=jnp.int32)
    flowing = upstream.astype(jnp.float32)
    along = jnp.sum(
        flowing[:, None, :] * picked.reshape(per_device, top, width).astype(jnp.float32), axis=2
    )
    grad_y = (
        (weights[:, :, None] * flowing[:, None, :])
        .astype(jnp.bfloat16)
        .reshape(per_device * top, width)
    )
    spread = jnp.zeros((experts * capacity, width), jnp.bfloat16).at[index].set(grad_y)
    grad_rows = expert_trade(spread.reshape(experts, capacity, width)).reshape(
        sources * capacity, width
    )
    gate = jnp.dot(arrived, gate_weight, preferred_element_type=jnp.float32)
    up_term = jnp.dot(arrived, up_weight, preferred_element_type=jnp.float32)
    active = jax.nn.silu(gate)
    inner = (active * up_term).astype(jnp.bfloat16)
    d_hidden = contract_last(grad_rows, down_weight)
    sigma = jax.nn.sigmoid(gate)
    d_gate = (d_hidden * up_term * sigma * (1.0 + gate * (1.0 - sigma))).astype(jnp.bfloat16)
    d_up = (d_hidden * active).astype(jnp.bfloat16)
    d_rows = (contract_last(d_gate, gate_weight) + contract_last(d_up, up_weight)).astype(
        jnp.bfloat16
    )
    returned = expert_trade(d_rows.reshape(sources, capacity, width)).reshape(
        experts * capacity, width
    )
    back = returned[index].reshape(per_device, top, width)
    grad_h = flowing + jnp.sum(back.astype(jnp.float32), axis=1)
    grad_s = weights * (along - jnp.sum(weights * along, axis=1, keepdims=True))
    match = chosen[:, :, None] == labels[None, None, :]
    grad_logits = jnp.sum(jnp.where(match, grad_s[:, :, None], 0.0), axis=1).astype(jnp.bfloat16)
    local_router = contract_first(hidden, grad_logits)
    grad_h = grad_h + contract_last(grad_logits, router_layer)
    passed = grad_h.astype(jnp.bfloat16)
    grads = (
        contract_first(arrived, d_gate),
        contract_first(arrived, d_up),
        contract_first(inner, grad_rows),
    )
    return passed, grads, local_router


def both_trade(first, second, shape):
    experts, capacity, sources, width = shape
    joined = jnp.concatenate(
        [first.reshape(experts, capacity, width), second.reshape(experts, capacity, width)], axis=1
    )
    traded = expert_trade(joined)
    return (
        traded[:, :capacity].reshape(sources * capacity, width),
        traded[:, capacity:].reshape(sources * capacity, width),
    )


def last_layer(hidden, upstream, chosen, router_layer, gate_weight, up_weight, down_weight, shape):
    experts, capacity, sources, width = shape
    per_device = hidden.shape[0]
    top = chosen.shape[1]
    labels = jnp.arange(experts, dtype=jnp.int32)
    weights = route_weights(hidden, chosen, router_layer)
    index = slot_index(chosen, experts, capacity)
    flowing = upstream.astype(jnp.float32)
    grad_y = (
        (weights[:, :, None] * flowing[:, None, :])
        .astype(jnp.bfloat16)
        .reshape(per_device * top, width)
    )
    spread = (
        jnp.zeros((experts * capacity, width), jnp.bfloat16)
        .at[index]
        .set(jnp.repeat(hidden, top, axis=0))
    )
    grad_spread = jnp.zeros((experts * capacity, width), jnp.bfloat16).at[index].set(grad_y)
    arrived, grad_rows = both_trade(spread, grad_spread, shape)
    gate = jnp.dot(arrived, gate_weight, preferred_element_type=jnp.float32)
    up_term = jnp.dot(arrived, up_weight, preferred_element_type=jnp.float32)
    active = jax.nn.silu(gate)
    inner = (active * up_term).astype(jnp.bfloat16)
    produced = jnp.dot(inner, down_weight, preferred_element_type=jnp.float32).astype(jnp.bfloat16)
    d_hidden = contract_last(grad_rows, down_weight)
    sigma = jax.nn.sigmoid(gate)
    d_gate = (d_hidden * up_term * sigma * (1.0 + gate * (1.0 - sigma))).astype(jnp.bfloat16)
    d_up = (d_hidden * active).astype(jnp.bfloat16)
    d_rows = (contract_last(d_gate, gate_weight) + contract_last(d_up, up_weight)).astype(
        jnp.bfloat16
    )
    grads = (
        contract_first(arrived, d_gate),
        contract_first(arrived, d_up),
        contract_first(inner, grad_rows),
    )
    returned, returned_grad = both_trade(produced, d_rows, shape)
    picked = returned[index].reshape(per_device, top, width).astype(jnp.float32)
    back = returned_grad[index].reshape(per_device, top, width)
    blended = jnp.sum(weights[:, :, None] * picked, axis=1)
    mixed = (hidden.astype(jnp.float32) + blended).astype(jnp.bfloat16)
    along = jnp.sum(flowing[:, None, :] * picked, axis=2)
    grad_h = flowing + jnp.sum(back.astype(jnp.float32), axis=1)
    grad_s = weights * (along - jnp.sum(weights * along, axis=1, keepdims=True))
    match = chosen[:, :, None] == labels[None, None, :]
    grad_logits = jnp.sum(jnp.where(match, grad_s[:, :, None], 0.0), axis=1).astype(jnp.bfloat16)
    local_router = contract_first(hidden, grad_logits)
    grad_h = grad_h + contract_last(grad_logits, router_layer)
    return mixed, grad_h.astype(jnp.bfloat16), grads, local_router


def shards(tokens, cotangent, routes, router, w_gate, w_up, w_down):
    sources = lax.axis_size("expert")
    groups = lax.axis_size("dp")
    section_id = lax.axis_index("section")
    batches, per_device, width = tokens.shape
    top = routes.shape[3]
    experts = router.shape[2]
    capacity = 3 * per_device * top // (2 * experts)
    shape = (experts, capacity, sources, width)
    layers = 2
    mine = section_id
    own = (router[0], w_gate[0, 0], w_up[0, 0], w_down[0, 0], fetch(routes[0], mine))
    other = swap((router[0], w_gate[0, 0], w_up[0, 0], w_down[0, 0], fetch(routes[0], 1 - mine)))
    params = [
        tuple(pick(section_id == layer, a, b) for a, b in zip(own, other)) for layer in range(layers)
    ]
    router_first, gate_first, up_first, down_first, chosen_first = params[0]
    router_last, gate_last, up_last, down_last, chosen_last = params[1]
    middle, kept = layer_forward(
        fetch(tokens, mine), chosen_first, router_first, gate_first, up_first, down_first, shape
    )
    final, upstream, grads_last, router_grad_last = last_layer(
        middle, fetch(cotangent, mine), chosen_last, router_last, gate_last, up_last, down_last, shape
    )
    passed_first, grads_first, router_grad_first = layer_backward(
        upstream, kept, chosen_first, router_first, gate_first, up_first, down_first, shape
    )
    outs = (middle, final)
    passed = (passed_first, upstream)
    grads = (grads_first, grads_last)
    routers = (router_grad_first, router_grad_last)
    first = section_id == 0

    def place(values):
        held = pick(first, values[0], values[1])
        sent = swap(pick(first, values[1], values[0]))
        return jnp.stack([pick(first, held, sent), pick(first, sent, held)])

    out_block = place(outs)
    grad_block = place(passed)
    own_grads = tuple(pick(first, a, b) for a, b in zip(grads[0], grads[1]))
    sent_grads = swap(
        tuple(pick(first, b, a).astype(jnp.bfloat16) for a, b in zip(grads[0], grads[1]))
    )
    whole_gate, whole_up, whole_down = (
        a + b.astype(jnp.float32) for a, b in zip(own_grads, sent_grads)
    )
    sum_gate, sum_up, sum_down = group_reduce(whole_gate, whole_up, whole_down, groups)
    own_router = pick(first, routers[0], routers[1])
    sum_router = own_router + swap(pick(first, routers[1], routers[0]))
    sum_router = device_reduce(sum_router, sources * groups)
    expert_scale = 1.0 / math.sqrt(batches * groups * per_device * top)
    router_scale = 1.0 / math.sqrt(batches * per_device * sources * groups)
    return (
        out_block[None],
        grad_block[None],
        (sum_gate * expert_scale)[None, None],
        (sum_up * expert_scale)[None, None],
        (sum_down * expert_scale)[None, None],
        (sum_router * router_scale)[None],
    )


def solution(mesh):
    placed = (
        P(None, ("expert", "dp"), None),
        P(None, ("expert", "dp"), None),
        P("section", None, ("expert", "dp"), None),
        P("section", None, None),
        P("section", "expert", None, None),
        P("section", "expert", None, None),
        P("section", "expert", None, None),
    )
    return jax.shard_map(
        shards,
        mesh=mesh,
        in_specs=placed,
        out_specs=(
            P("section", None, ("expert", "dp"), None),
            P("section", None, ("expert", "dp"), None),
            P("section", "expert", "dp", None),
            P("section", "expert", "dp", None),
            P("section", "expert", "dp", None),
            P("section", None, None),
        ),
        check_vma=False,
    )
```

```python
import math

import jax
import jax.numpy as jnp
from jax import lax
from jax.sharding import PartitionSpec as P


def from_behind(array, axis, by):
    length = lax.axis_size(axis)
    pairs = [(i, i + by) for i in range(length) if 0 <= i + by < length]
    return lax.ppermute(array, axis, pairs)


def contract_last(left, right):
    return lax.dot_general(
        left, right, (((1,), (1,)), ((), ())), preferred_element_type=jnp.float32
    )


def contract_first(left, right):
    return lax.dot_general(
        left, right, (((0,), (0,)), ((), ())), preferred_element_type=jnp.float32
    )


def slot_index(chosen, experts, capacity):
    flat = chosen.reshape(-1)
    labels = jnp.arange(experts, dtype=jnp.int32)
    onehot = (flat[:, None] == labels[None, :]).astype(jnp.int32)
    before = jnp.cumsum(onehot, axis=0) - onehot
    position = jnp.sum(before * onehot, axis=1)
    return flat * capacity + position


def route_weights(hidden, chosen, router_layer):
    logits = jnp.dot(hidden, router_layer, preferred_element_type=jnp.float32)
    labels = jnp.arange(logits.shape[1], dtype=jnp.int32)
    match = chosen[:, :, None] == labels[None, None, :]
    picked = jnp.sum(jnp.where(match, logits[:, None, :], 0.0), axis=2)
    raised = jnp.exp(picked)
    return raised / jnp.sum(raised, axis=1, keepdims=True)


def expert_trade(block):
    return lax.all_to_all(block, "expert", split_axis=0, concat_axis=0, tiled=True)


def fetch(store, place):
    return lax.dynamic_index_in_dim(store, place, 0, keepdims=False)


def store_at(store, value, place, valid):
    previous = fetch(store, place)
    return lax.dynamic_update_index_in_dim(store, jnp.where(valid, value, previous), place, 0)


def group_reduce(whole_gate, whole_up, whole_down, rider, groups):
    parts = [part.reshape(groups, -1).astype(jnp.bfloat16) for part in (whole_gate, whole_up, whole_down)]
    spread = jnp.broadcast_to(rider.reshape(1, -1).astype(jnp.bfloat16), (groups, rider.size))
    stacked = jnp.concatenate(parts + [spread], axis=1)
    traded = lax.all_to_all(stacked, "dp", 0, 0, tiled=True)
    summed = jnp.sum(traded.astype(jnp.float32), axis=0)
    sizes = [part.shape[1] for part in parts]
    cuts = [0, sizes[0], sizes[0] + sizes[1], sizes[0] + sizes[1] + sizes[2]]
    rows_gate = whole_gate.shape[0] // groups
    rows_down = whole_down.shape[0] // groups
    return (
        summed[cuts[0] : cuts[1]].reshape(rows_gate, whole_gate.shape[1]),
        summed[cuts[1] : cuts[2]].reshape(rows_gate, whole_up.shape[1]),
        summed[cuts[2] : cuts[3]].reshape(rows_down, whole_down.shape[1]),
        summed[cuts[3] :].reshape(rider.shape),
    )


def device_reduce(value, count):
    chunks = value.reshape(count, -1, value.shape[1])
    traded = lax.all_to_all(chunks, ("expert", "dp"), 0, 0, tiled=True)
    total = jnp.sum(traded, axis=0, keepdims=True)
    spread = jnp.broadcast_to(total, chunks.shape)
    return lax.all_to_all(spread, ("expert", "dp"), 0, 0, tiled=True).reshape(value.shape)


def swap(array):
    return lax.ppermute(array, "section", [(0, 1), (1, 0)])


def pick(flag, first, second):
    return jnp.where(flag, first, second)


def layer_forward(hidden, chosen, router_layer, gate_weight, up_weight, down_weight, shape):
    experts, capacity, sources, width = shape
    per_device = hidden.shape[0]
    top = chosen.shape[1]
    weights = route_weights(hidden, chosen, router_layer)
    index = slot_index(chosen, experts, capacity)
    spread = (
        jnp.zeros((experts * capacity, width), jnp.bfloat16)
        .at[index]
        .set(jnp.repeat(hidden, top, axis=0))
    )
    arrived = expert_trade(spread.reshape(experts, capacity, width)).reshape(
        sources * capacity, width
    )
    gate = jnp.dot(arrived, gate_weight, preferred_element_type=jnp.float32)
    up_term = jnp.dot(arrived, up_weight, preferred_element_type=jnp.float32)
    inner = (jax.nn.silu(gate) * up_term).astype(jnp.bfloat16)
    produced = jnp.dot(inner, down_weight, preferred_element_type=jnp.float32).astype(jnp.bfloat16)
    returned = expert_trade(produced.reshape(sources, capacity, width)).reshape(
        experts * capacity, width
    )
    picked = returned[index]
    blended = jnp.sum(
        weights[:, :, None] * picked.reshape(per_device, top, width).astype(jnp.float32), axis=1
    )
    mixed = (hidden.astype(jnp.float32) + blended).astype(jnp.bfloat16)
    return mixed, (hidden, picked, arrived, weights, index)


def layer_backward(upstream, saved, chosen, router_layer, gate_weight, up_weight, down_weight, shape):
    experts, capacity, sources, width = shape
    hidden, picked, arrived, weights, index = saved
    per_device = hidden.shape[0]
    top = chosen.shape[1]
    labels = jnp.arange(experts, dtype=jnp.int32)
    flowing = upstream.astype(jnp.float32)
    along = jnp.sum(
        flowing[:, None, :] * picked.reshape(per_device, top, width).astype(jnp.float32), axis=2
    )
    grad_y = (
        (weights[:, :, None] * flowing[:, None, :])
        .astype(jnp.bfloat16)
        .reshape(per_device * top, width)
    )
    spread = jnp.zeros((experts * capacity, width), jnp.bfloat16).at[index].set(grad_y)
    grad_rows = expert_trade(spread.reshape(experts, capacity, width)).reshape(
        sources * capacity, width
    )
    gate = jnp.dot(arrived, gate_weight, preferred_element_type=jnp.float32)
    up_term = jnp.dot(arrived, up_weight, preferred_element_type=jnp.float32)
    active = jax.nn.silu(gate)
    inner = (active * up_term).astype(jnp.bfloat16)
    d_hidden = contract_last(grad_rows, down_weight)
    sigma = jax.nn.sigmoid(gate)
    d_gate = (d_hidden * up_term * sigma * (1.0 + gate * (1.0 - sigma))).astype(jnp.bfloat16)
    d_up = (d_hidden * active).astype(jnp.bfloat16)
    d_rows = (contract_last(d_gate, gate_weight) + contract_last(d_up, up_weight)).astype(
        jnp.bfloat16
    )
    returned = expert_trade(d_rows.reshape(sources, capacity, width)).reshape(
        experts * capacity, width
    )
    back = returned[index].reshape(per_device, top, width)
    grad_h = flowing + jnp.sum(back.astype(jnp.float32), axis=1)
    grad_s = weights * (along - jnp.sum(weights * along, axis=1, keepdims=True))
    match = chosen[:, :, None] == labels[None, None, :]
    grad_logits = jnp.sum(jnp.where(match, grad_s[:, :, None], 0.0), axis=1).astype(jnp.bfloat16)
    local_router = contract_first(hidden, grad_logits)
    grad_h = grad_h + contract_last(grad_logits, router_layer)
    passed = grad_h.astype(jnp.bfloat16)
    grads = (
        contract_first(arrived, d_gate),
        contract_first(arrived, d_up),
        contract_first(inner, grad_rows),
    )
    return passed, grads, local_router


def both_trade(first, second, shape):
    experts, capacity, sources, width = shape
    joined = jnp.concatenate(
        [first.reshape(experts, capacity, width), second.reshape(experts, capacity, width)], axis=1
    )
    traded = expert_trade(joined)
    return (
        traded[:, :capacity].reshape(sources * capacity, width),
        traded[:, capacity:].reshape(sources * capacity, width),
    )


def last_layer(hidden, upstream, chosen, router_layer, gate_weight, up_weight, down_weight, shape):
    experts, capacity, sources, width = shape
    per_device = hidden.shape[0]
    top = chosen.shape[1]
    labels = jnp.arange(experts, dtype=jnp.int32)
    weights = route_weights(hidden, chosen, router_layer)
    index = slot_index(chosen, experts, capacity)
    flowing = upstream.astype(jnp.float32)
    grad_y = (
        (weights[:, :, None] * flowing[:, None, :])
        .astype(jnp.bfloat16)
        .reshape(per_device * top, width)
    )
    spread = (
        jnp.zeros((experts * capacity, width), jnp.bfloat16)
        .at[index]
        .set(jnp.repeat(hidden, top, axis=0))
    )
    grad_spread = jnp.zeros((experts * capacity, width), jnp.bfloat16).at[index].set(grad_y)
    arrived, grad_rows = both_trade(spread, grad_spread, shape)
    gate = jnp.dot(arrived, gate_weight, preferred_element_type=jnp.float32)
    up_term = jnp.dot(arrived, up_weight, preferred_element_type=jnp.float32)
    active = jax.nn.silu(gate)
    inner = (active * up_term).astype(jnp.bfloat16)
    produced = jnp.dot(inner, down_weight, preferred_element_type=jnp.float32).astype(jnp.bfloat16)
    d_hidden = contract_last(grad_rows, down_weight)
    sigma = jax.nn.sigmoid(gate)
    d_gate = (d_hidden * up_term * sigma * (1.0 + gate * (1.0 - sigma))).astype(jnp.bfloat16)
    d_up = (d_hidden * active).astype(jnp.bfloat16)
    d_rows = (contract_last(d_gate, gate_weight) + contract_last(d_up, up_weight)).astype(
        jnp.bfloat16
    )
    grads = (
        contract_first(arrived, d_gate),
        contract_first(arrived, d_up),
        contract_first(inner, grad_rows),
    )
    returned, returned_grad = both_trade(produced, d_rows, shape)
    picked = returned[index].reshape(per_device, top, width).astype(jnp.float32)
    back = returned_grad[index].reshape(per_device, top, width)
    blended = jnp.sum(weights[:, :, None] * picked, axis=1)
    mixed = (hidden.astype(jnp.float32) + blended).astype(jnp.bfloat16)
    along = jnp.sum(flowing[:, None, :] * picked, axis=2)
    grad_h = flowing + jnp.sum(back.astype(jnp.float32), axis=1)
    grad_s = weights * (along - jnp.sum(weights * along, axis=1, keepdims=True))
    match = chosen[:, :, None] == labels[None, None, :]
    grad_logits = jnp.sum(jnp.where(match, grad_s[:, :, None], 0.0), axis=1).astype(jnp.bfloat16)
    local_router = contract_first(hidden, grad_logits)
    grad_h = grad_h + contract_last(grad_logits, router_layer)
    return mixed, grad_h.astype(jnp.bfloat16), grads, local_router


def first_backward(upstream, saved, chosen, params, shape, router_last, first):
    router_layer, gate_weight, up_weight, down_weight = params
    experts, capacity, sources, width = shape
    hidden, picked, arrived, weights, index = saved
    per_device = hidden.shape[0]
    top = chosen.shape[1]
    labels = jnp.arange(experts, dtype=jnp.int32)
    flowing = upstream.astype(jnp.float32)
    along = jnp.sum(
        flowing[:, None, :] * picked.reshape(per_device, top, width).astype(jnp.float32), axis=2
    )
    grad_s = weights * (along - jnp.sum(weights * along, axis=1, keepdims=True))
    match = chosen[:, :, None] == labels[None, None, :]
    grad_logits = jnp.sum(jnp.where(match, grad_s[:, :, None], 0.0), axis=1).astype(jnp.bfloat16)
    local_router = contract_first(hidden, grad_logits)
    router_sum = pick(first, local_router, router_last) + swap(
        pick(first, router_last, local_router)
    )
    riders = router_sum.reshape(sources, -1, width).astype(jnp.bfloat16)
    grad_y = (
        (weights[:, :, None] * flowing[:, None, :])
        .astype(jnp.bfloat16)
        .reshape(per_device * top, width)
    )
    spread = jnp.zeros((experts * capacity, width), jnp.bfloat16).at[index].set(grad_y)
    traded = expert_trade(
        jnp.concatenate([spread.reshape(experts, capacity, width), riders], axis=1)
    )
    grad_rows = traded[:, :capacity].reshape(sources * capacity, width)
    partial = jnp.sum(traded[:, capacity:].astype(jnp.float32), axis=0)
    gate = jnp.dot(arrived, gate_weight, preferred_element_type=jnp.float32)
    up_term = jnp.dot(arrived, up_weight, preferred_element_type=jnp.float32)
    active = jax.nn.silu(gate)
    inner = (active * up_term).astype(jnp.bfloat16)
    d_hidden = contract_last(grad_rows, down_weight)
    sigma = jax.nn.sigmoid(gate)
    d_gate = (d_hidden * up_term * sigma * (1.0 + gate * (1.0 - sigma))).astype(jnp.bfloat16)
    d_up = (d_hidden * active).astype(jnp.bfloat16)
    d_rows = (contract_last(d_gate, gate_weight) + contract_last(d_up, up_weight)).astype(
        jnp.bfloat16
    )
    back_riders = jnp.broadcast_to(partial.astype(jnp.bfloat16)[None], (sources,) + partial.shape)
    returned_all = expert_trade(
        jnp.concatenate([d_rows.reshape(sources, capacity, width), back_riders], axis=1)
    )
    returned = returned_all[:, :capacity].reshape(experts * capacity, width)
    router_grad = returned_all[:, capacity:].astype(jnp.float32).reshape(router_sum.shape)
    back = returned[index].reshape(per_device, top, width)
    grad_h = flowing + jnp.sum(back.astype(jnp.float32), axis=1)
    grad_h = grad_h + contract_last(grad_logits, router_layer)
    passed = grad_h.astype(jnp.bfloat16)
    grads = (
        contract_first(arrived, d_gate),
        contract_first(arrived, d_up),
        contract_first(inner, grad_rows),
    )
    return passed, grads, router_grad


def shards(tokens, cotangent, routes, router, w_gate, w_up, w_down):
    sources = lax.axis_size("expert")
    groups = lax.axis_size("dp")
    section_id = lax.axis_index("section")
    batches, per_device, width = tokens.shape
    top = routes.shape[3]
    experts = router.shape[2]
    capacity = 3 * per_device * top // (2 * experts)
    shape = (experts, capacity, sources, width)
    layers = 2
    mine = section_id
    own = (router[0], w_gate[0, 0], w_up[0, 0], w_down[0, 0], fetch(routes[0], mine))
    other = swap((router[0], w_gate[0, 0], w_up[0, 0], w_down[0, 0], fetch(routes[0], 1 - mine)))
    params = [
        tuple(pick(section_id == layer, a, b) for a, b in zip(own, other)) for layer in range(layers)
    ]
    router_first, gate_first, up_first, down_first, chosen_first = params[0]
    router_last, gate_last, up_last, down_last, chosen_last = params[1]
    middle, kept = layer_forward(
        fetch(tokens, mine), chosen_first, router_first, gate_first, up_first, down_first, shape
    )
    final, upstream, grads_last, router_grad_last = last_layer(
        middle, fetch(cotangent, mine), chosen_last, router_last, gate_last, up_last, down_last, shape
    )
    first = section_id == 0
    passed_first, grads_first, router_grad = first_backward(
        upstream,
        kept,
        chosen_first,
        (router_first, gate_first, up_first, down_first),
        shape,
        router_grad_last,
        first,
    )
    outs = (middle, final)
    passed = (passed_first, upstream)
    grads = (grads_first, grads_last)

    def place(values):
        held = pick(first, values[0], values[1])
        sent = swap(pick(first, values[1], values[0]))
        return jnp.stack([pick(first, held, sent), pick(first, sent, held)])

    out_block = place(outs)
    grad_block = place(passed)
    own_grads = tuple(pick(first, a, b) for a, b in zip(grads[0], grads[1]))
    sent_grads = swap(
        tuple(pick(first, b, a).astype(jnp.bfloat16) for a, b in zip(grads[0], grads[1]))
    )
    whole_gate, whole_up, whole_down = (
        a + b.astype(jnp.float32) for a, b in zip(own_grads, sent_grads)
    )
    sum_gate, sum_up, sum_down, sum_router = group_reduce(
        whole_gate, whole_up, whole_down, router_grad, groups
    )
    expert_scale = 1.0 / math.sqrt(batches * groups * per_device * top)
    router_scale = 1.0 / math.sqrt(batches * per_device * sources * groups)
    return (
        out_block[None],
        grad_block[None],
        (sum_gate * expert_scale)[None, None],
        (sum_up * expert_scale)[None, None],
        (sum_down * expert_scale)[None, None],
        (sum_router * router_scale)[None],
    )


def solution(mesh):
    placed = (
        P(None, ("expert", "dp"), None),
        P(None, ("expert", "dp"), None),
        P("section", None, ("expert", "dp"), None),
        P("section", None, None),
        P("section", "expert", None, None),
        P("section", "expert", None, None),
        P("section", "expert", None, None),
    )
    return jax.shard_map(
        shards,
        mesh=mesh,
        in_specs=placed,
        out_specs=(
            P("section", None, ("expert", "dp"), None),
            P("section", None, ("expert", "dp"), None),
            P("section", "expert", "dp", None),
            P("section", "expert", "dp", None),
            P("section", "expert", "dp", None),
            P("section", None, None),
        ),
        check_vma=False,
    )
```

```python
import math

import jax
import jax.numpy as jnp
from jax import lax
from jax.sharding import PartitionSpec as P


def from_behind(array, axis, by):
    length = lax.axis_size(axis)
    pairs = [(i, i + by) for i in range(length) if 0 <= i + by < length]
    return lax.ppermute(array, axis, pairs)


def contract_last(left, right):
    return lax.dot_general(
        left, right, (((1,), (1,)), ((), ())), preferred_element_type=jnp.float32
    )


def contract_first(left, right):
    return lax.dot_general(
        left, right, (((0,), (0,)), ((), ())), preferred_element_type=jnp.float32
    )


def slot_index(chosen, experts, capacity):
    flat = chosen.reshape(-1)
    labels = jnp.arange(experts, dtype=jnp.int32)
    onehot = (flat[:, None] == labels[None, :]).astype(jnp.int32)
    before = jnp.cumsum(onehot, axis=0) - onehot
    position = jnp.sum(before * onehot, axis=1)
    return flat * capacity + position


def route_weights(hidden, chosen, router_layer):
    logits = jnp.dot(hidden, router_layer, preferred_element_type=jnp.float32)
    labels = jnp.arange(logits.shape[1], dtype=jnp.int32)
    match = chosen[:, :, None] == labels[None, None, :]
    picked = jnp.sum(jnp.where(match, logits[:, None, :], 0.0), axis=2)
    raised = jnp.exp(picked)
    return raised / jnp.sum(raised, axis=1, keepdims=True)


def expert_trade(block):
    return lax.all_to_all(block, "expert", split_axis=0, concat_axis=0, tiled=True)


def fetch(store, place):
    return lax.dynamic_index_in_dim(store, place, 0, keepdims=False)


def store_at(store, value, place, valid):
    previous = fetch(store, place)
    return lax.dynamic_update_index_in_dim(store, jnp.where(valid, value, previous), place, 0)


def group_reduce(whole_gate, whole_up, whole_down, rider, groups):
    rows_gate = whole_gate.shape[0] // groups
    rows_down = whole_down.shape[0] // groups
    width = whole_down.shape[1]
    half = whole_gate.shape[1]
    paired = jnp.concatenate(
        [whole_gate.reshape(groups, rows_gate, half), whole_up.reshape(groups, rows_gate, half)],
        axis=2,
    )
    spread = jnp.broadcast_to(rider[None], (groups,) + rider.shape)
    stacked = jnp.concatenate(
        [
            paired.astype(jnp.bfloat16),
            whole_down.reshape(groups, rows_down, width).astype(jnp.bfloat16),
            spread.astype(jnp.bfloat16),
        ],
        axis=1,
    )
    traded = lax.all_to_all(stacked, "dp", 0, 0, tiled=True)
    summed = jnp.sum(traded.astype(jnp.float32), axis=0)
    return (
        summed[:rows_gate, :half],
        summed[:rows_gate, half:],
        summed[rows_gate : rows_gate + rows_down],
        summed[rows_gate + rows_down :],
    )


def device_reduce(value, count):
    chunks = value.reshape(count, -1, value.shape[1])
    traded = lax.all_to_all(chunks, ("expert", "dp"), 0, 0, tiled=True)
    total = jnp.sum(traded, axis=0, keepdims=True)
    spread = jnp.broadcast_to(total, chunks.shape)
    return lax.all_to_all(spread, ("expert", "dp"), 0, 0, tiled=True).reshape(value.shape)


def swap(array):
    return lax.ppermute(array, "section", [(0, 1), (1, 0)])


def pick(flag, first, second):
    return jnp.where(flag, first, second)


def layer_forward(hidden, chosen, router_layer, gate_weight, up_weight, down_weight, shape):
    experts, capacity, sources, width = shape
    per_device = hidden.shape[0]
    top = chosen.shape[1]
    weights = route_weights(hidden, chosen, router_layer)
    index = slot_index(chosen, experts, capacity)
    spread = (
        jnp.zeros((experts * capacity, width), jnp.bfloat16)
        .at[index]
        .set(jnp.repeat(hidden, top, axis=0))
    )
    arrived = expert_trade(spread.reshape(experts, capacity, width)).reshape(
        sources * capacity, width
    )
    gate = jnp.dot(arrived, gate_weight, preferred_element_type=jnp.float32)
    up_term = jnp.dot(arrived, up_weight, preferred_element_type=jnp.float32)
    inner = (jax.nn.silu(gate) * up_term).astype(jnp.bfloat16)
    produced = jnp.dot(inner, down_weight, preferred_element_type=jnp.float32).astype(jnp.bfloat16)
    returned = expert_trade(produced.reshape(sources, capacity, width)).reshape(
        experts * capacity, width
    )
    picked = returned[index]
    blended = jnp.sum(
        weights[:, :, None] * picked.reshape(per_device, top, width).astype(jnp.float32), axis=1
    )
    mixed = (hidden.astype(jnp.float32) + blended).astype(jnp.bfloat16)
    return mixed, (hidden, picked, arrived, weights, index)


def layer_backward(upstream, saved, chosen, router_layer, gate_weight, up_weight, down_weight, shape):
    experts, capacity, sources, width = shape
    hidden, picked, arrived, weights, index = saved
    per_device = hidden.shape[0]
    top = chosen.shape[1]
    labels = jnp.arange(experts, dtype=jnp.int32)
    flowing = upstream.astype(jnp.float32)
    along = jnp.sum(
        flowing[:, None, :] * picked.reshape(per_device, top, width).astype(jnp.float32), axis=2
    )
    grad_y = (
        (weights[:, :, None] * flowing[:, None, :])
        .astype(jnp.bfloat16)
        .reshape(per_device * top, width)
    )
    spread = jnp.zeros((experts * capacity, width), jnp.bfloat16).at[index].set(grad_y)
    grad_rows = expert_trade(spread.reshape(experts, capacity, width)).reshape(
        sources * capacity, width
    )
    gate = jnp.dot(arrived, gate_weight, preferred_element_type=jnp.float32)
    up_term = jnp.dot(arrived, up_weight, preferred_element_type=jnp.float32)
    active = jax.nn.silu(gate)
    inner = (active * up_term).astype(jnp.bfloat16)
    d_hidden = contract_last(grad_rows, down_weight)
    sigma = jax.nn.sigmoid(gate)
    d_gate = (d_hidden * up_term * sigma * (1.0 + gate * (1.0 - sigma))).astype(jnp.bfloat16)
    d_up = (d_hidden * active).astype(jnp.bfloat16)
    d_rows = (contract_last(d_gate, gate_weight) + contract_last(d_up, up_weight)).astype(
        jnp.bfloat16
    )
    returned = expert_trade(d_rows.reshape(sources, capacity, width)).reshape(
        experts * capacity, width
    )
    back = returned[index].reshape(per_device, top, width)
    grad_h = flowing + jnp.sum(back.astype(jnp.float32), axis=1)
    grad_s = weights * (along - jnp.sum(weights * along, axis=1, keepdims=True))
    match = chosen[:, :, None] == labels[None, None, :]
    grad_logits = jnp.sum(jnp.where(match, grad_s[:, :, None], 0.0), axis=1).astype(jnp.bfloat16)
    local_router = contract_first(hidden, grad_logits)
    grad_h = grad_h + contract_last(grad_logits, router_layer)
    passed = grad_h.astype(jnp.bfloat16)
    grads = (
        contract_first(arrived, d_gate),
        contract_first(arrived, d_up),
        contract_first(inner, grad_rows),
    )
    return passed, grads, local_router


def both_trade(first, second, shape):
    experts, capacity, sources, width = shape
    joined = jnp.concatenate(
        [first.reshape(experts, capacity, width), second.reshape(experts, capacity, width)], axis=1
    )
    traded = expert_trade(joined)
    return (
        traded[:, :capacity].reshape(sources * capacity, width),
        traded[:, capacity:].reshape(sources * capacity, width),
    )


def last_layer(hidden, upstream, chosen, router_layer, gate_weight, up_weight, down_weight, shape):
    experts, capacity, sources, width = shape
    per_device = hidden.shape[0]
    top = chosen.shape[1]
    labels = jnp.arange(experts, dtype=jnp.int32)
    weights = route_weights(hidden, chosen, router_layer)
    index = slot_index(chosen, experts, capacity)
    flowing = upstream.astype(jnp.float32)
    grad_y = (
        (weights[:, :, None] * flowing[:, None, :])
        .astype(jnp.bfloat16)
        .reshape(per_device * top, width)
    )
    spread = (
        jnp.zeros((experts * capacity, width), jnp.bfloat16)
        .at[index]
        .set(jnp.repeat(hidden, top, axis=0))
    )
    grad_spread = jnp.zeros((experts * capacity, width), jnp.bfloat16).at[index].set(grad_y)
    arrived, grad_rows = both_trade(spread, grad_spread, shape)
    gate = jnp.dot(arrived, gate_weight, preferred_element_type=jnp.float32)
    up_term = jnp.dot(arrived, up_weight, preferred_element_type=jnp.float32)
    active = jax.nn.silu(gate)
    inner = (active * up_term).astype(jnp.bfloat16)
    produced = jnp.dot(inner, down_weight, preferred_element_type=jnp.float32).astype(jnp.bfloat16)
    d_hidden = contract_last(grad_rows, down_weight)
    sigma = jax.nn.sigmoid(gate)
    d_gate = (d_hidden * up_term * sigma * (1.0 + gate * (1.0 - sigma))).astype(jnp.bfloat16)
    d_up = (d_hidden * active).astype(jnp.bfloat16)
    d_rows = (contract_last(d_gate, gate_weight) + contract_last(d_up, up_weight)).astype(
        jnp.bfloat16
    )
    grads = (
        contract_first(arrived, d_gate),
        contract_first(arrived, d_up),
        contract_first(inner, grad_rows),
    )
    returned, returned_grad = both_trade(produced, d_rows, shape)
    picked = returned[index].reshape(per_device, top, width).astype(jnp.float32)
    back = returned_grad[index].reshape(per_device, top, width)
    blended = jnp.sum(weights[:, :, None] * picked, axis=1)
    mixed = (hidden.astype(jnp.float32) + blended).astype(jnp.bfloat16)
    along = jnp.sum(flowing[:, None, :] * picked, axis=2)
    grad_h = flowing + jnp.sum(back.astype(jnp.float32), axis=1)
    grad_s = weights * (along - jnp.sum(weights * along, axis=1, keepdims=True))
    match = chosen[:, :, None] == labels[None, None, :]
    grad_logits = jnp.sum(jnp.where(match, grad_s[:, :, None], 0.0), axis=1).astype(jnp.bfloat16)
    local_router = contract_first(hidden, grad_logits)
    grad_h = grad_h + contract_last(grad_logits, router_layer)
    return mixed, grad_h.astype(jnp.bfloat16), grads, local_router


def first_backward(upstream, saved, chosen, params, shape, router_last, first):
    router_layer, gate_weight, up_weight, down_weight = params
    experts, capacity, sources, width = shape
    hidden, picked, arrived, weights, index = saved
    per_device = hidden.shape[0]
    top = chosen.shape[1]
    labels = jnp.arange(experts, dtype=jnp.int32)
    flowing = upstream.astype(jnp.float32)
    along = jnp.sum(
        flowing[:, None, :] * picked.reshape(per_device, top, width).astype(jnp.float32), axis=2
    )
    grad_s = weights * (along - jnp.sum(weights * along, axis=1, keepdims=True))
    match = chosen[:, :, None] == labels[None, None, :]
    grad_logits = jnp.sum(jnp.where(match, grad_s[:, :, None], 0.0), axis=1).astype(jnp.bfloat16)
    local_router = contract_first(hidden, grad_logits)
    router_sum = pick(first, local_router, router_last) + swap(
        pick(first, router_last, local_router)
    )
    riders = router_sum.reshape(sources, -1, width).astype(jnp.bfloat16)
    grad_y = (
        (weights[:, :, None] * flowing[:, None, :])
        .astype(jnp.bfloat16)
        .reshape(per_device * top, width)
    )
    spread = jnp.zeros((experts * capacity, width), jnp.bfloat16).at[index].set(grad_y)
    traded = expert_trade(
        jnp.concatenate([spread.reshape(experts, capacity, width), riders], axis=1)
    )
    grad_rows = traded[:, :capacity].reshape(sources * capacity, width)
    partial = jnp.sum(traded[:, capacity:].astype(jnp.float32), axis=0)
    gate = jnp.dot(arrived, gate_weight, preferred_element_type=jnp.float32)
    up_term = jnp.dot(arrived, up_weight, preferred_element_type=jnp.float32)
    active = jax.nn.silu(gate)
    inner = (active * up_term).astype(jnp.bfloat16)
    d_hidden = contract_last(grad_rows, down_weight)
    sigma = jax.nn.sigmoid(gate)
    d_gate = (d_hidden * up_term * sigma * (1.0 + gate * (1.0 - sigma))).astype(jnp.bfloat16)
    d_up = (d_hidden * active).astype(jnp.bfloat16)
    d_rows = (contract_last(d_gate, gate_weight) + contract_last(d_up, up_weight)).astype(
        jnp.bfloat16
    )
    back_riders = jnp.broadcast_to(partial.astype(jnp.bfloat16)[None], (sources,) + partial.shape)
    returned_all = expert_trade(
        jnp.concatenate([d_rows.reshape(sources, capacity, width), back_riders], axis=1)
    )
    returned = returned_all[:, :capacity].reshape(experts * capacity, width)
    router_grad = returned_all[:, capacity:].reshape(sources, -1)
    back = returned[index].reshape(per_device, top, width)
    grad_h = flowing + jnp.sum(back.astype(jnp.float32), axis=1)
    grad_h = grad_h + contract_last(grad_logits, router_layer)
    passed = grad_h.astype(jnp.bfloat16)
    grads = (
        contract_first(arrived, d_gate),
        contract_first(arrived, d_up),
        contract_first(inner, grad_rows),
    )
    return passed, grads, router_grad


def shards(tokens, cotangent, routes, router, w_gate, w_up, w_down):
    sources = lax.axis_size("expert")
    groups = lax.axis_size("dp")
    section_id = lax.axis_index("section")
    batches, per_device, width = tokens.shape
    top = routes.shape[3]
    experts = router.shape[2]
    capacity = 3 * per_device * top // (2 * experts)
    shape = (experts, capacity, sources, width)
    layers = 2
    mine = section_id
    own = (router[0], w_gate[0, 0], w_up[0, 0], w_down[0, 0], fetch(routes[0], mine))
    other = swap((router[0], w_gate[0, 0], w_up[0, 0], w_down[0, 0], fetch(routes[0], 1 - mine)))
    params = [
        tuple(pick(section_id == layer, a, b) for a, b in zip(own, other)) for layer in range(layers)
    ]
    router_first, gate_first, up_first, down_first, chosen_first = params[0]
    router_last, gate_last, up_last, down_last, chosen_last = params[1]
    middle, kept = layer_forward(
        fetch(tokens, mine), chosen_first, router_first, gate_first, up_first, down_first, shape
    )
    final, upstream, grads_last, router_grad_last = last_layer(
        middle, fetch(cotangent, mine), chosen_last, router_last, gate_last, up_last, down_last, shape
    )
    first = section_id == 0
    passed_first, grads_first, router_grad = first_backward(
        upstream,
        kept,
        chosen_first,
        (router_first, gate_first, up_first, down_first),
        shape,
        router_grad_last,
        first,
    )
    outs = (middle, final)
    passed = (passed_first, upstream)
    grads = (grads_first, grads_last)

    def place(values):
        held = pick(first, values[0], values[1])
        sent = swap(pick(first, values[1], values[0]))
        return jnp.stack([pick(first, held, sent), pick(first, sent, held)])

    out_block = place(outs)
    grad_block = place(passed)
    own_grads = tuple(pick(first, a, b) for a, b in zip(grads[0], grads[1]))
    sent_grads = swap(
        tuple(pick(first, b, a).astype(jnp.bfloat16) for a, b in zip(grads[0], grads[1]))
    )
    whole_gate, whole_up, whole_down = (
        a + b.astype(jnp.float32) for a, b in zip(own_grads, sent_grads)
    )
    sum_gate, sum_up, sum_down, sum_router = group_reduce(
        whole_gate, whole_up, whole_down, router_grad, groups
    )
    expert_scale = 1.0 / math.sqrt(batches * groups * per_device * top)
    router_scale = 1.0 / math.sqrt(batches * per_device * sources * groups)
    return (
        out_block[None],
        grad_block[None],
        (sum_gate * expert_scale)[None, None],
        (sum_up * expert_scale)[None, None],
        (sum_down * expert_scale)[None, None],
        (sum_router * router_scale).reshape(router.shape[1:])[None],
    )


def solution(mesh):
    placed = (
        P(None, ("expert", "dp"), None),
        P(None, ("expert", "dp"), None),
        P("section", None, ("expert", "dp"), None),
        P("section", None, None),
        P("section", "expert", None, None),
        P("section", "expert", None, None),
        P("section", "expert", None, None),
    )
    return jax.shard_map(
        shards,
        mesh=mesh,
        in_specs=placed,
        out_specs=(
            P("section", None, ("expert", "dp"), None),
            P("section", None, ("expert", "dp"), None),
            P("section", "expert", "dp", None),
            P("section", "expert", "dp", None),
            P("section", "expert", "dp", None),
            P("section", None, None),
        ),
        check_vma=False,
    )
```

```python
import math

import jax
import jax.numpy as jnp
from jax import lax
from jax.sharding import PartitionSpec as P


def from_behind(array, axis, by):
    length = lax.axis_size(axis)
    pairs = [(i, i + by) for i in range(length) if 0 <= i + by < length]
    return lax.ppermute(array, axis, pairs)


def contract_last(left, right):
    return lax.dot_general(
        left, right, (((1,), (1,)), ((), ())), preferred_element_type=jnp.float32
    )


def contract_first(left, right):
    return lax.dot_general(
        left, right, (((0,), (0,)), ((), ())), preferred_element_type=jnp.float32
    )


def slot_index(chosen, experts, capacity):
    flat = chosen.reshape(-1)
    labels = jnp.arange(experts, dtype=jnp.int32)
    onehot = (flat[:, None] == labels[None, :]).astype(jnp.int32)
    before = jnp.cumsum(onehot, axis=0) - onehot
    position = jnp.sum(before * onehot, axis=1)
    return flat * capacity + position


def route_weights(hidden, chosen, router_layer):
    logits = jnp.dot(hidden, router_layer, preferred_element_type=jnp.float32)
    labels = jnp.arange(logits.shape[1], dtype=jnp.int32)
    match = chosen[:, :, None] == labels[None, None, :]
    picked = jnp.sum(jnp.where(match, logits[:, None, :], 0.0), axis=2)
    raised = jnp.exp(picked)
    return raised / jnp.sum(raised, axis=1, keepdims=True)


def expert_trade(block):
    return lax.all_to_all(block, "expert", split_axis=0, concat_axis=0, tiled=True)


def fetch(store, place):
    return lax.dynamic_index_in_dim(store, place, 0, keepdims=False)


def store_at(store, value, place, valid):
    previous = fetch(store, place)
    return lax.dynamic_update_index_in_dim(store, jnp.where(valid, value, previous), place, 0)


def group_reduce(whole_gate, whole_up, whole_down, rider, groups):
    rows_gate = whole_gate.shape[0] // groups
    rows_down = whole_down.shape[0] // groups
    width = whole_down.shape[1]
    half = whole_gate.shape[1]
    paired = jnp.concatenate(
        [whole_gate.reshape(groups, rows_gate, half), whole_up.reshape(groups, rows_gate, half)],
        axis=2,
    )
    spread = jnp.broadcast_to(rider[None], (groups,) + rider.shape)
    stacked = jnp.concatenate(
        [
            paired.astype(jnp.bfloat16),
            whole_down.reshape(groups, rows_down, width).astype(jnp.bfloat16),
            spread.astype(jnp.bfloat16),
        ],
        axis=1,
    )
    traded = lax.all_to_all(stacked, "dp", 0, 0, tiled=True)
    summed = jnp.sum(traded.astype(jnp.float32), axis=0)
    return (
        summed[:rows_gate, :half],
        summed[:rows_gate, half:],
        summed[rows_gate : rows_gate + rows_down],
        summed[rows_gate + rows_down :],
    )


def device_reduce(value, count):
    chunks = value.reshape(count, -1, value.shape[1])
    traded = lax.all_to_all(chunks, ("expert", "dp"), 0, 0, tiled=True)
    total = jnp.sum(traded, axis=0, keepdims=True)
    spread = jnp.broadcast_to(total, chunks.shape)
    return lax.all_to_all(spread, ("expert", "dp"), 0, 0, tiled=True).reshape(value.shape)


def swap(array):
    return lax.ppermute(array, "section", [(0, 1), (1, 0)])


def pick(flag, first, second):
    return jnp.where(flag, first, second)


def layer_forward(hidden, chosen, router_layer, gate_weight, up_weight, down_weight, shape):
    experts, capacity, sources, width = shape
    per_device = hidden.shape[0]
    top = chosen.shape[1]
    weights = route_weights(hidden, chosen, router_layer)
    index = slot_index(chosen, experts, capacity)
    spread = (
        jnp.zeros((experts * capacity, width), jnp.bfloat16)
        .at[index]
        .set(jnp.repeat(hidden, top, axis=0))
    )
    arrived = expert_trade(spread.reshape(experts, capacity, width)).reshape(
        sources * capacity, width
    )
    gate = jnp.dot(arrived, gate_weight, preferred_element_type=jnp.float32)
    up_term = jnp.dot(arrived, up_weight, preferred_element_type=jnp.float32)
    inner = (jax.nn.silu(gate) * up_term).astype(jnp.bfloat16)
    produced = jnp.dot(inner, down_weight, preferred_element_type=jnp.float32).astype(jnp.bfloat16)
    returned = expert_trade(produced.reshape(sources, capacity, width)).reshape(
        experts * capacity, width
    )
    picked = returned[index]
    blended = jnp.sum(
        weights[:, :, None] * picked.reshape(per_device, top, width).astype(jnp.float32), axis=1
    )
    mixed = (hidden.astype(jnp.float32) + blended).astype(jnp.bfloat16)
    return mixed, (hidden, picked, arrived, weights, index)


def layer_backward(upstream, saved, chosen, router_layer, gate_weight, up_weight, down_weight, shape):
    experts, capacity, sources, width = shape
    hidden, picked, arrived, weights, index = saved
    per_device = hidden.shape[0]
    top = chosen.shape[1]
    labels = jnp.arange(experts, dtype=jnp.int32)
    flowing = upstream.astype(jnp.float32)
    along = jnp.sum(
        flowing[:, None, :] * picked.reshape(per_device, top, width).astype(jnp.float32), axis=2
    )
    grad_y = (
        (weights[:, :, None] * flowing[:, None, :])
        .astype(jnp.bfloat16)
        .reshape(per_device * top, width)
    )
    spread = jnp.zeros((experts * capacity, width), jnp.bfloat16).at[index].set(grad_y)
    grad_rows = expert_trade(spread.reshape(experts, capacity, width)).reshape(
        sources * capacity, width
    )
    gate = jnp.dot(arrived, gate_weight, preferred_element_type=jnp.float32)
    up_term = jnp.dot(arrived, up_weight, preferred_element_type=jnp.float32)
    active = jax.nn.silu(gate)
    inner = (active * up_term).astype(jnp.bfloat16)
    d_hidden = contract_last(grad_rows, down_weight)
    sigma = jax.nn.sigmoid(gate)
    d_gate = (d_hidden * up_term * sigma * (1.0 + gate * (1.0 - sigma))).astype(jnp.bfloat16)
    d_up = (d_hidden * active).astype(jnp.bfloat16)
    d_rows = (contract_last(d_gate, gate_weight) + contract_last(d_up, up_weight)).astype(
        jnp.bfloat16
    )
    returned = expert_trade(d_rows.reshape(sources, capacity, width)).reshape(
        experts * capacity, width
    )
    back = returned[index].reshape(per_device, top, width)
    grad_h = flowing + jnp.sum(back.astype(jnp.float32), axis=1)
    grad_s = weights * (along - jnp.sum(weights * along, axis=1, keepdims=True))
    match = chosen[:, :, None] == labels[None, None, :]
    grad_logits = jnp.sum(jnp.where(match, grad_s[:, :, None], 0.0), axis=1).astype(jnp.bfloat16)
    local_router = contract_first(hidden, grad_logits)
    grad_h = grad_h + contract_last(grad_logits, router_layer)
    passed = grad_h.astype(jnp.bfloat16)
    grads = (
        contract_first(arrived, d_gate),
        contract_first(arrived, d_up),
        contract_first(inner, grad_rows),
    )
    return passed, grads, local_router


def both_trade(first, second, shape):
    experts, capacity, sources, width = shape
    joined = jnp.concatenate(
        [first.reshape(experts, capacity, width), second.reshape(experts, capacity, width)], axis=1
    )
    traded = expert_trade(joined)
    return (
        traded[:, :capacity].reshape(sources * capacity, width),
        traded[:, capacity:].reshape(sources * capacity, width),
    )


def last_layer(hidden, upstream, chosen, router_layer, gate_weight, up_weight, down_weight, shape):
    experts, capacity, sources, width = shape
    per_device = hidden.shape[0]
    top = chosen.shape[1]
    labels = jnp.arange(experts, dtype=jnp.int32)
    weights = route_weights(hidden, chosen, router_layer)
    index = slot_index(chosen, experts, capacity)
    flowing = upstream.astype(jnp.float32)
    grad_y = (
        (weights[:, :, None] * flowing[:, None, :])
        .astype(jnp.bfloat16)
        .reshape(per_device * top, width)
    )
    spread = (
        jnp.zeros((experts * capacity, width), jnp.bfloat16)
        .at[index]
        .set(jnp.repeat(hidden, top, axis=0))
    )
    grad_spread = jnp.zeros((experts * capacity, width), jnp.bfloat16).at[index].set(grad_y)
    arrived, grad_rows = both_trade(spread, grad_spread, shape)
    gate = jnp.dot(arrived, gate_weight, preferred_element_type=jnp.float32)
    up_term = jnp.dot(arrived, up_weight, preferred_element_type=jnp.float32)
    active = jax.nn.silu(gate)
    inner = (active * up_term).astype(jnp.bfloat16)
    produced = jnp.dot(inner, down_weight, preferred_element_type=jnp.float32).astype(jnp.bfloat16)
    d_hidden = contract_last(grad_rows, down_weight)
    sigma = jax.nn.sigmoid(gate)
    d_gate = (d_hidden * up_term * sigma * (1.0 + gate * (1.0 - sigma))).astype(jnp.bfloat16)
    d_up = (d_hidden * active).astype(jnp.bfloat16)
    d_rows = (contract_last(d_gate, gate_weight) + contract_last(d_up, up_weight)).astype(
        jnp.bfloat16
    )
    grads = (
        contract_first(arrived, d_gate),
        contract_first(arrived, d_up),
        contract_first(inner, grad_rows),
    )
    returned, returned_grad = both_trade(produced, d_rows, shape)
    picked = returned[index].reshape(per_device, top, width).astype(jnp.float32)
    back = returned_grad[index].reshape(per_device, top, width)
    blended = jnp.sum(weights[:, :, None] * picked, axis=1)
    mixed = (hidden.astype(jnp.float32) + blended).astype(jnp.bfloat16)
    along = jnp.sum(flowing[:, None, :] * picked, axis=2)
    grad_h = flowing + jnp.sum(back.astype(jnp.float32), axis=1)
    grad_s = weights * (along - jnp.sum(weights * along, axis=1, keepdims=True))
    match = chosen[:, :, None] == labels[None, None, :]
    grad_logits = jnp.sum(jnp.where(match, grad_s[:, :, None], 0.0), axis=1).astype(jnp.bfloat16)
    local_router = contract_first(hidden, grad_logits)
    grad_h = grad_h + contract_last(grad_logits, router_layer)
    return mixed, grad_h.astype(jnp.bfloat16), grads, local_router


def first_backward(upstream, saved, chosen, params, shape, router_last, first, rider_row):
    router_layer, gate_weight, up_weight, down_weight = params
    experts, capacity, sources, width = shape
    hidden, picked, arrived, weights, index = saved
    per_device = hidden.shape[0]
    top = chosen.shape[1]
    labels = jnp.arange(experts, dtype=jnp.int32)
    flowing = upstream.astype(jnp.float32)
    along = jnp.sum(
        flowing[:, None, :] * picked.reshape(per_device, top, width).astype(jnp.float32), axis=2
    )
    grad_s = weights * (along - jnp.sum(weights * along, axis=1, keepdims=True))
    match = chosen[:, :, None] == labels[None, None, :]
    grad_logits = jnp.sum(jnp.where(match, grad_s[:, :, None], 0.0), axis=1).astype(jnp.bfloat16)
    local_router = contract_first(hidden, grad_logits)
    router_sum = pick(first, local_router, router_last) + swap(
        pick(first, router_last, local_router)
    )
    riders = router_sum.reshape(sources, width).astype(jnp.bfloat16)
    grad_y = (
        (weights[:, :, None] * flowing[:, None, :])
        .astype(jnp.bfloat16)
        .reshape(per_device * top, width)
    )
    spread = jnp.zeros((experts * capacity, width), jnp.bfloat16).at[index].set(grad_y)
    spread = spread.reshape(experts, capacity, width).at[:, rider_row].set(riders)
    traded = expert_trade(spread)
    row_ids = lax.broadcasted_iota(jnp.int32, traded.shape, 1)
    grad_rows = jnp.where(row_ids == rider_row, jnp.zeros_like(traded), traded).reshape(
        sources * capacity, width
    )
    partial = jnp.sum(traded[:, rider_row].astype(jnp.float32), axis=0)
    gate = jnp.dot(arrived, gate_weight, preferred_element_type=jnp.float32)
    up_term = jnp.dot(arrived, up_weight, preferred_element_type=jnp.float32)
    active = jax.nn.silu(gate)
    inner = (active * up_term).astype(jnp.bfloat16)
    d_hidden = contract_last(grad_rows, down_weight)
    sigma = jax.nn.sigmoid(gate)
    d_gate = (d_hidden * up_term * sigma * (1.0 + gate * (1.0 - sigma))).astype(jnp.bfloat16)
    d_up = (d_hidden * active).astype(jnp.bfloat16)
    d_rows = (contract_last(d_gate, gate_weight) + contract_last(d_up, up_weight)).astype(
        jnp.bfloat16
    )
    back_riders = jnp.broadcast_to(partial.astype(jnp.bfloat16)[None], (sources,) + partial.shape)
    returned_all = expert_trade(
        d_rows.reshape(sources, capacity, width).at[:, rider_row].set(back_riders)
    )
    returned = returned_all.reshape(experts * capacity, width)
    router_grad = returned_all[:, rider_row]
    back = returned[index].reshape(per_device, top, width)
    grad_h = flowing + jnp.sum(back.astype(jnp.float32), axis=1)
    grad_h = grad_h + contract_last(grad_logits, router_layer)
    passed = grad_h.astype(jnp.bfloat16)
    grads = (
        contract_first(arrived, d_gate),
        contract_first(arrived, d_up),
        contract_first(inner, grad_rows),
    )
    return passed, grads, router_grad


def shards(tokens, cotangent, routes, router, w_gate, w_up, w_down):
    sources = lax.axis_size("expert")
    groups = lax.axis_size("dp")
    section_id = lax.axis_index("section")
    batches, per_device, width = tokens.shape
    top = routes.shape[3]
    experts = router.shape[2]
    capacity = 3 * per_device * top // (2 * experts)
    slots = (capacity + 16) // 16 * 16
    shape = (experts, slots, sources, width)
    layers = 2
    mine = section_id
    own = (router[0], w_gate[0, 0], w_up[0, 0], w_down[0, 0], fetch(routes[0], mine))
    other = swap((router[0], w_gate[0, 0], w_up[0, 0], w_down[0, 0], fetch(routes[0], 1 - mine)))
    params = [
        tuple(pick(section_id == layer, a, b) for a, b in zip(own, other)) for layer in range(layers)
    ]
    router_first, gate_first, up_first, down_first, chosen_first = params[0]
    router_last, gate_last, up_last, down_last, chosen_last = params[1]
    middle, kept = layer_forward(
        fetch(tokens, mine), chosen_first, router_first, gate_first, up_first, down_first, shape
    )
    final, upstream, grads_last, router_grad_last = last_layer(
        middle, fetch(cotangent, mine), chosen_last, router_last, gate_last, up_last, down_last, shape
    )
    first = section_id == 0
    passed_first, grads_first, router_grad = first_backward(
        upstream,
        kept,
        chosen_first,
        (router_first, gate_first, up_first, down_first),
        shape,
        router_grad_last,
        first,
        capacity,
    )
    outs = (middle, final)
    passed = (passed_first, upstream)
    grads = (grads_first, grads_last)

    def place(values):
        held = pick(first, values[0], values[1])
        sent = swap(pick(first, values[1], values[0]))
        return jnp.stack([pick(first, held, sent), pick(first, sent, held)])

    out_block = place(outs)
    grad_block = place(passed)
    own_grads = tuple(pick(first, a, b) for a, b in zip(grads[0], grads[1]))
    sent_grads = swap(
        tuple(pick(first, b, a).astype(jnp.bfloat16) for a, b in zip(grads[0], grads[1]))
    )
    whole_gate, whole_up, whole_down = (
        a + b.astype(jnp.float32) for a, b in zip(own_grads, sent_grads)
    )
    sum_gate, sum_up, sum_down, sum_router = group_reduce(
        whole_gate, whole_up, whole_down, router_grad, groups
    )
    expert_scale = 1.0 / math.sqrt(batches * groups * per_device * top)
    router_scale = 1.0 / math.sqrt(batches * per_device * sources * groups)
    return (
        out_block[None],
        grad_block[None],
        (sum_gate * expert_scale)[None, None],
        (sum_up * expert_scale)[None, None],
        (sum_down * expert_scale)[None, None],
        (sum_router * router_scale).reshape(router.shape[1:])[None],
    )


def solution(mesh):
    placed = (
        P(None, ("expert", "dp"), None),
        P(None, ("expert", "dp"), None),
        P("section", None, ("expert", "dp"), None),
        P("section", None, None),
        P("section", "expert", None, None),
        P("section", "expert", None, None),
        P("section", "expert", None, None),
    )
    return jax.shard_map(
        shards,
        mesh=mesh,
        in_specs=placed,
        out_specs=(
            P("section", None, ("expert", "dp"), None),
            P("section", None, ("expert", "dp"), None),
            P("section", "expert", "dp", None),
            P("section", "expert", "dp", None),
            P("section", "expert", "dp", None),
            P("section", None, None),
        ),
        check_vma=False,
    )
```

```python
import math

import jax
import jax.numpy as jnp
from jax import lax
from jax.sharding import PartitionSpec as P


def from_behind(array, axis, by):
    length = lax.axis_size(axis)
    pairs = [(i, i + by) for i in range(length) if 0 <= i + by < length]
    return lax.ppermute(array, axis, pairs)


def contract_last(left, right):
    return lax.dot_general(
        left, right, (((1,), (1,)), ((), ())), preferred_element_type=jnp.float32
    )


def contract_first(left, right):
    return lax.dot_general(
        left, right, (((0,), (0,)), ((), ())), preferred_element_type=jnp.float32
    )


def slot_index(chosen, experts, capacity):
    flat = chosen.reshape(-1)
    labels = jnp.arange(experts, dtype=jnp.int32)
    onehot = (flat[:, None] == labels[None, :]).astype(jnp.int32)
    before = jnp.cumsum(onehot, axis=0) - onehot
    position = jnp.sum(before * onehot, axis=1)
    return flat * capacity + position


def route_weights(hidden, chosen, router_layer):
    logits = jnp.dot(hidden, router_layer, preferred_element_type=jnp.float32)
    labels = jnp.arange(logits.shape[1], dtype=jnp.int32)
    match = chosen[:, :, None] == labels[None, None, :]
    picked = jnp.sum(jnp.where(match, logits[:, None, :], 0.0), axis=2)
    raised = jnp.exp(picked)
    return raised / jnp.sum(raised, axis=1, keepdims=True)


def expert_trade(block):
    return lax.all_to_all(block, "expert", split_axis=0, concat_axis=0, tiled=True)


def fetch(store, place):
    return lax.dynamic_index_in_dim(store, place, 0, keepdims=False)


def store_at(store, value, place, valid):
    previous = fetch(store, place)
    return lax.dynamic_update_index_in_dim(store, jnp.where(valid, value, previous), place, 0)


def group_reduce(whole_gate, whole_up, whole_down, rider, groups):
    rows_gate = whole_gate.shape[0] // groups
    rows_down = whole_down.shape[0] // groups
    width = whole_down.shape[1]
    half = whole_gate.shape[1]
    paired = jnp.concatenate(
        [whole_gate.reshape(groups, rows_gate, half), whole_up.reshape(groups, rows_gate, half)],
        axis=2,
    )
    spread = jnp.broadcast_to(rider[None], (groups,) + rider.shape)
    stacked = jnp.concatenate(
        [
            paired.astype(jnp.bfloat16),
            whole_down.reshape(groups, rows_down, width).astype(jnp.bfloat16),
            spread.astype(jnp.bfloat16),
        ],
        axis=1,
    )
    traded = lax.all_to_all(stacked, "dp", 0, 0, tiled=True)
    summed = jnp.sum(traded.astype(jnp.float32), axis=0)
    return (
        summed[:rows_gate, :half],
        summed[:rows_gate, half:],
        summed[rows_gate : rows_gate + rows_down],
        summed[rows_gate + rows_down :],
    )


def device_reduce(value, count):
    chunks = value.reshape(count, -1, value.shape[1])
    traded = lax.all_to_all(chunks, ("expert", "dp"), 0, 0, tiled=True)
    total = jnp.sum(traded, axis=0, keepdims=True)
    spread = jnp.broadcast_to(total, chunks.shape)
    return lax.all_to_all(spread, ("expert", "dp"), 0, 0, tiled=True).reshape(value.shape)


def swap(array):
    return lax.ppermute(array, "section", [(0, 1), (1, 0)])


def pick(flag, first, second):
    return jnp.where(flag, first, second)


def layer_forward(hidden, chosen, router_layer, gate_weight, up_weight, down_weight, shape):
    experts, capacity, sources, width = shape
    per_device = hidden.shape[0]
    top = chosen.shape[1]
    weights = route_weights(hidden, chosen, router_layer)
    index = slot_index(chosen, experts, capacity)
    spread = (
        jnp.zeros((experts * capacity, width), jnp.bfloat16)
        .at[index]
        .set(jnp.repeat(hidden, top, axis=0))
    )
    arrived = expert_trade(spread.reshape(experts, capacity, width)).reshape(
        sources * capacity, width
    )
    gate = jnp.dot(arrived, gate_weight, preferred_element_type=jnp.float32)
    up_term = jnp.dot(arrived, up_weight, preferred_element_type=jnp.float32)
    inner = (jax.nn.silu(gate) * up_term).astype(jnp.bfloat16)
    produced = jnp.dot(inner, down_weight, preferred_element_type=jnp.float32).astype(jnp.bfloat16)
    returned = expert_trade(produced.reshape(sources, capacity, width)).reshape(
        experts * capacity, width
    )
    picked = returned[index]
    blended = jnp.sum(
        weights[:, :, None] * picked.reshape(per_device, top, width).astype(jnp.float32), axis=1
    )
    mixed = (hidden.astype(jnp.float32) + blended).astype(jnp.bfloat16)
    return mixed, (hidden, picked, arrived, weights, index)


def layer_backward(upstream, saved, chosen, router_layer, gate_weight, up_weight, down_weight, shape):
    experts, capacity, sources, width = shape
    hidden, picked, arrived, weights, index = saved
    per_device = hidden.shape[0]
    top = chosen.shape[1]
    labels = jnp.arange(experts, dtype=jnp.int32)
    flowing = upstream.astype(jnp.float32)
    along = jnp.sum(
        flowing[:, None, :] * picked.reshape(per_device, top, width).astype(jnp.float32), axis=2
    )
    grad_y = (
        (weights[:, :, None] * flowing[:, None, :])
        .astype(jnp.bfloat16)
        .reshape(per_device * top, width)
    )
    spread = jnp.zeros((experts * capacity, width), jnp.bfloat16).at[index].set(grad_y)
    grad_rows = expert_trade(spread.reshape(experts, capacity, width)).reshape(
        sources * capacity, width
    )
    gate = jnp.dot(arrived, gate_weight, preferred_element_type=jnp.float32)
    up_term = jnp.dot(arrived, up_weight, preferred_element_type=jnp.float32)
    active = jax.nn.silu(gate)
    inner = (active * up_term).astype(jnp.bfloat16)
    d_hidden = contract_last(grad_rows, down_weight)
    sigma = jax.nn.sigmoid(gate)
    d_gate = (d_hidden * up_term * sigma * (1.0 + gate * (1.0 - sigma))).astype(jnp.bfloat16)
    d_up = (d_hidden * active).astype(jnp.bfloat16)
    d_rows = (contract_last(d_gate, gate_weight) + contract_last(d_up, up_weight)).astype(
        jnp.bfloat16
    )
    returned = expert_trade(d_rows.reshape(sources, capacity, width)).reshape(
        experts * capacity, width
    )
    back = returned[index].reshape(per_device, top, width)
    grad_h = flowing + jnp.sum(back.astype(jnp.float32), axis=1)
    grad_s = weights * (along - jnp.sum(weights * along, axis=1, keepdims=True))
    match = chosen[:, :, None] == labels[None, None, :]
    grad_logits = jnp.sum(jnp.where(match, grad_s[:, :, None], 0.0), axis=1).astype(jnp.bfloat16)
    local_router = contract_first(hidden, grad_logits)
    grad_h = grad_h + contract_last(grad_logits, router_layer)
    passed = grad_h.astype(jnp.bfloat16)
    grads = (
        contract_first(arrived, d_gate),
        contract_first(arrived, d_up),
        contract_first(inner, grad_rows),
    )
    return passed, grads, local_router


def both_trade(first, second, shape, used):
    experts, capacity, sources, width = shape
    joined = jnp.concatenate(
        [
            first.reshape(experts, capacity, width)[:, :used],
            second.reshape(experts, capacity, width)[:, :used],
        ],
        axis=1,
    )
    traded = expert_trade(joined)
    spare = ((0, 0), (0, capacity - used), (0, 0))
    return (
        jnp.pad(traded[:, :used], spare).reshape(sources * capacity, width),
        jnp.pad(traded[:, used:], spare).reshape(sources * capacity, width),
    )


def last_layer(hidden, upstream, chosen, params, shape, used):
    router_layer, gate_weight, up_weight, down_weight = params
    experts, capacity, sources, width = shape
    per_device = hidden.shape[0]
    top = chosen.shape[1]
    labels = jnp.arange(experts, dtype=jnp.int32)
    weights = route_weights(hidden, chosen, router_layer)
    index = slot_index(chosen, experts, capacity)
    flowing = upstream.astype(jnp.float32)
    grad_y = (
        (weights[:, :, None] * flowing[:, None, :])
        .astype(jnp.bfloat16)
        .reshape(per_device * top, width)
    )
    spread = (
        jnp.zeros((experts * capacity, width), jnp.bfloat16)
        .at[index]
        .set(jnp.repeat(hidden, top, axis=0))
    )
    grad_spread = jnp.zeros((experts * capacity, width), jnp.bfloat16).at[index].set(grad_y)
    arrived, grad_rows = both_trade(spread, grad_spread, shape, used)
    gate = jnp.dot(arrived, gate_weight, preferred_element_type=jnp.float32)
    up_term = jnp.dot(arrived, up_weight, preferred_element_type=jnp.float32)
    active = jax.nn.silu(gate)
    inner = (active * up_term).astype(jnp.bfloat16)
    produced = jnp.dot(inner, down_weight, preferred_element_type=jnp.float32).astype(jnp.bfloat16)
    d_hidden = contract_last(grad_rows, down_weight)
    sigma = jax.nn.sigmoid(gate)
    d_gate = (d_hidden * up_term * sigma * (1.0 + gate * (1.0 - sigma))).astype(jnp.bfloat16)
    d_up = (d_hidden * active).astype(jnp.bfloat16)
    d_rows = (contract_last(d_gate, gate_weight) + contract_last(d_up, up_weight)).astype(
        jnp.bfloat16
    )
    grads = (
        contract_first(arrived, d_gate),
        contract_first(arrived, d_up),
        contract_first(inner, grad_rows),
    )
    returned, returned_grad = both_trade(produced, d_rows, shape, used)
    picked = returned[index].reshape(per_device, top, width).astype(jnp.float32)
    back = returned_grad[index].reshape(per_device, top, width)
    blended = jnp.sum(weights[:, :, None] * picked, axis=1)
    mixed = (hidden.astype(jnp.float32) + blended).astype(jnp.bfloat16)
    along = jnp.sum(flowing[:, None, :] * picked, axis=2)
    grad_h = flowing + jnp.sum(back.astype(jnp.float32), axis=1)
    grad_s = weights * (along - jnp.sum(weights * along, axis=1, keepdims=True))
    match = chosen[:, :, None] == labels[None, None, :]
    grad_logits = jnp.sum(jnp.where(match, grad_s[:, :, None], 0.0), axis=1).astype(jnp.bfloat16)
    local_router = contract_first(hidden, grad_logits)
    grad_h = grad_h + contract_last(grad_logits, router_layer)
    return mixed, grad_h.astype(jnp.bfloat16), grads, local_router


def first_backward(upstream, saved, chosen, params, shape, router_last, first, rider_row):
    router_layer, gate_weight, up_weight, down_weight = params
    experts, capacity, sources, width = shape
    hidden, picked, arrived, weights, index = saved
    per_device = hidden.shape[0]
    top = chosen.shape[1]
    labels = jnp.arange(experts, dtype=jnp.int32)
    flowing = upstream.astype(jnp.float32)
    along = jnp.sum(
        flowing[:, None, :] * picked.reshape(per_device, top, width).astype(jnp.float32), axis=2
    )
    grad_s = weights * (along - jnp.sum(weights * along, axis=1, keepdims=True))
    match = chosen[:, :, None] == labels[None, None, :]
    grad_logits = jnp.sum(jnp.where(match, grad_s[:, :, None], 0.0), axis=1).astype(jnp.bfloat16)
    local_router = contract_first(hidden, grad_logits)
    router_sum = pick(first, local_router, router_last) + swap(
        pick(first, router_last, local_router)
    )
    riders = router_sum.reshape(sources, width).astype(jnp.bfloat16)
    grad_y = (
        (weights[:, :, None] * flowing[:, None, :])
        .astype(jnp.bfloat16)
        .reshape(per_device * top, width)
    )
    spread = jnp.zeros((experts * capacity, width), jnp.bfloat16).at[index].set(grad_y)
    spread = spread.reshape(experts, capacity, width).at[:, rider_row].set(riders)
    traded = expert_trade(spread)
    row_ids = lax.broadcasted_iota(jnp.int32, traded.shape, 1)
    grad_rows = jnp.where(row_ids == rider_row, jnp.zeros_like(traded), traded).reshape(
        sources * capacity, width
    )
    partial = jnp.sum(traded[:, rider_row].astype(jnp.float32), axis=0)
    gate = jnp.dot(arrived, gate_weight, preferred_element_type=jnp.float32)
    up_term = jnp.dot(arrived, up_weight, preferred_element_type=jnp.float32)
    active = jax.nn.silu(gate)
    inner = (active * up_term).astype(jnp.bfloat16)
    d_hidden = contract_last(grad_rows, down_weight)
    sigma = jax.nn.sigmoid(gate)
    d_gate = (d_hidden * up_term * sigma * (1.0 + gate * (1.0 - sigma))).astype(jnp.bfloat16)
    d_up = (d_hidden * active).astype(jnp.bfloat16)
    d_rows = (contract_last(d_gate, gate_weight) + contract_last(d_up, up_weight)).astype(
        jnp.bfloat16
    )
    back_riders = jnp.broadcast_to(partial.astype(jnp.bfloat16)[None], (sources,) + partial.shape)
    returned_all = expert_trade(
        d_rows.reshape(sources, capacity, width).at[:, rider_row].set(back_riders)
    )
    returned = returned_all.reshape(experts * capacity, width)
    router_grad = returned_all[:, rider_row]
    back = returned[index].reshape(per_device, top, width)
    grad_h = flowing + jnp.sum(back.astype(jnp.float32), axis=1)
    grad_h = grad_h + contract_last(grad_logits, router_layer)
    passed = grad_h.astype(jnp.bfloat16)
    grads = (
        contract_first(arrived, d_gate),
        contract_first(arrived, d_up),
        contract_first(inner, grad_rows),
    )
    return passed, grads, router_grad


def shards(tokens, cotangent, routes, router, w_gate, w_up, w_down):
    sources = lax.axis_size("expert")
    groups = lax.axis_size("dp")
    section_id = lax.axis_index("section")
    batches, per_device, width = tokens.shape
    top = routes.shape[3]
    experts = router.shape[2]
    capacity = 3 * per_device * top // (2 * experts)
    slots = (capacity + 16) // 16 * 16
    shape = (experts, slots, sources, width)
    layers = 2
    mine = section_id
    own = (router[0], w_gate[0, 0], w_up[0, 0], w_down[0, 0], fetch(routes[0], mine))
    other = swap((router[0], w_gate[0, 0], w_up[0, 0], w_down[0, 0], fetch(routes[0], 1 - mine)))
    params = [
        tuple(pick(section_id == layer, a, b) for a, b in zip(own, other)) for layer in range(layers)
    ]
    router_first, gate_first, up_first, down_first, chosen_first = params[0]
    router_last, gate_last, up_last, down_last, chosen_last = params[1]
    middle, kept = layer_forward(
        fetch(tokens, mine), chosen_first, router_first, gate_first, up_first, down_first, shape
    )
    final, upstream, grads_last, router_grad_last = last_layer(
        middle,
        fetch(cotangent, mine),
        chosen_last,
        (router_last, gate_last, up_last, down_last),
        shape,
        capacity,
    )
    first = section_id == 0
    passed_first, grads_first, router_grad = first_backward(
        upstream,
        kept,
        chosen_first,
        (router_first, gate_first, up_first, down_first),
        shape,
        router_grad_last,
        first,
        capacity,
    )
    outs = (middle, final)
    passed = (passed_first, upstream)
    grads = (grads_first, grads_last)

    def place(values):
        held = pick(first, values[0], values[1])
        sent = swap(pick(first, values[1], values[0]))
        return jnp.stack([pick(first, held, sent), pick(first, sent, held)])

    out_block = place(outs)
    grad_block = place(passed)
    own_grads = tuple(pick(first, a, b) for a, b in zip(grads[0], grads[1]))
    sent_grads = swap(
        tuple(pick(first, b, a).astype(jnp.bfloat16) for a, b in zip(grads[0], grads[1]))
    )
    whole_gate, whole_up, whole_down = (
        a + b.astype(jnp.float32) for a, b in zip(own_grads, sent_grads)
    )
    sum_gate, sum_up, sum_down, sum_router = group_reduce(
        whole_gate, whole_up, whole_down, router_grad, groups
    )
    expert_scale = 1.0 / math.sqrt(batches * groups * per_device * top)
    router_scale = 1.0 / math.sqrt(batches * per_device * sources * groups)
    return (
        out_block[None],
        grad_block[None],
        (sum_gate * expert_scale)[None, None],
        (sum_up * expert_scale)[None, None],
        (sum_down * expert_scale)[None, None],
        (sum_router * router_scale).reshape(router.shape[1:])[None],
    )


def solution(mesh):
    placed = (
        P(None, ("expert", "dp"), None),
        P(None, ("expert", "dp"), None),
        P("section", None, ("expert", "dp"), None),
        P("section", None, None),
        P("section", "expert", None, None),
        P("section", "expert", None, None),
        P("section", "expert", None, None),
    )
    return jax.shard_map(
        shards,
        mesh=mesh,
        in_specs=placed,
        out_specs=(
            P("section", None, ("expert", "dp"), None),
            P("section", None, ("expert", "dp"), None),
            P("section", "expert", "dp", None),
            P("section", "expert", "dp", None),
            P("section", "expert", "dp", None),
            P("section", None, None),
        ),
        check_vma=False,
    )
```
